256 devices in a mesh: seq: 64 (over y_lo, x, z), fsdp: 4 (over y_hi, core).
Axes of the slice: x: 4, y: 4 (y_hi: 2, y_lo: 2; y = y_hi * 2 + y_lo), z: 8, core: 2. Of those that a mesh axis runs over, the one named last changes fastest.
Arguments:
- inputs: bfloat16 [4, 16384, 1536], P(None, ('seq', 'fsdp')), may hold values from -6 to 6
- cotangent: bfloat16 [4, 16384, 1536], P(None, ('seq', 'fsdp')), may hold values from -24 to 24
- dilated_kernel_weight: bfloat16 [1536, 3, 768], P('seq', None, 'fsdp'), may hold values from -0.09375 to 0.09375
- point_weight: bfloat16 [1536, 768], P('seq', 'fsdp'), may hold values from -0.21875 to 0.21875
Outputs:
- outputs: bfloat16 [4, 16384, 1536], P(None, ('seq', 'fsdp'))
- grad_inputs: bfloat16 [4, 16384, 1536], P(None, ('seq', 'fsdp'))
- grad_conv: float32 [1536, 3, 768], P('seq', None, 'fsdp')
- grad_point: float32 [1536, 768], P('seq', 'fsdp')
The draws below stay inside these ranges and needn't reach their ends.
All inputs are finite; a program needn't handle non-finite values.
Results may differ from the reference program's by a relative error of at most 0.0053.
Values may be sent and summed in bfloat16 or wider, within the bound.
No kernel may reach another device: no remote copies, remote signals or barrier semaphores. Data moves between devices by JAX's collectives and lax.ppermute only.
A program may use at most 128 MiB of HBM per device.

```python
import math
import jax
import jax.numpy as jnp
from jax import lax

C = 1536
CH = 768
SEQS = 4
DILATION_BINS = 128
BINS = 16384


def raised(array, key, source, target, blocks, factor):
    owner, partner = [(jnp.arange(array.shape[axis_at]) // (array.shape[axis_at] // blocks)).reshape([-1 if axis == axis_at else 1 for axis in range(array.ndim)]) for axis_at in (source, target)]
    chosen = jax.random.permutation(key, blocks)[partner]
    strong = (owner == chosen) | (owner == (partner + blocks // 2) % blocks)
    return jnp.where(strong, factor * array, array)


def level_of(own_key, shape, cuts, smallest, largest):
    gain, own = 1.0, jax.random.fold_in(own_key, 6)
    for axis_at, blocks in cuts:
        draws = jnp.exp(jax.random.uniform(jax.random.fold_in(own, axis_at), (blocks,), jnp.float32, smallest / len(cuts), largest / len(cuts)))
        gain = gain * jnp.repeat(draws, shape[axis_at] // blocks).reshape([-1 if axis == axis_at else 1 for axis in range(len(shape))])
    return gain


def bell_draw(own_key, shape, width, reach, pieces=(), held_as=jnp.bfloat16):
    entries = width * jax.random.normal(own_key, shape, jnp.float32)
    if pieces:
        entries = entries * level_of(own_key, shape, pieces, -0.22, 0.18)
    return jnp.clip(entries, -reach, reach).astype(held_as)


def bell_draw_with(stream_key, dims, width, bound, pieces, heavy, kind=jnp.bfloat16):
    values = width * jax.random.normal(stream_key, dims, jnp.float32)
    if pieces:
        values = values * level_of(stream_key, dims, pieces, -0.22, 0.18)
    return jnp.clip(raised(values, jax.random.fold_in(stream_key, 3), *heavy), -bound, bound).astype(kind)


def setup_inputs(seed: int = 0) -> dict:
    streams_of = jax.random.split(jax.random.key(seed), 5)
    inputs = bell_draw(streams_of[0], (SEQS, BINS, C), 1.0, 6.0, ((1, 256),))
    cotangent = bell_draw_with(streams_of[1], (SEQS, BINS, C), 1.0, 24.0, ((1, 256),), (1, 2, 256, 6.0))
    dilated_kernel_weight = bell_draw(streams_of[2], (C, 3, CH), (3 * C) ** -0.5, 0.09375, ((0, 64), (2, 4)))
    point_weight = bell_draw(streams_of[3], (C, CH), CH ** -0.5, 0.21875, ((0, 64), (1, 4)))
    return dict(inputs=inputs, cotangent=cotangent, dilated_kernel_weight=dilated_kernel_weight, point_weight=point_weight)


def gelu_value(v):
    return 0.5 * v * (1.0 + lax.erf(v * (1.0 / math.sqrt(2.0))))

def gelu_slope(v):
    return 0.5 * (1.0 + lax.erf(v * (1.0 / math.sqrt(2.0)))) + v * jnp.exp(-0.5 * v * v) * (1.0 / math.sqrt(2.0 * math.pi))

def shifted_bin_rows(field, offset):
    zeros = jnp.zeros((field.shape[0], abs(offset), field.shape[2]), field.dtype)
    if offset > 0:
        return jnp.concatenate([zeros, field[:, :-offset]], axis=1)
    return jnp.concatenate([field[:, -offset:], zeros], axis=1)

def reference(inputs, cotangent, dilated_kernel_weight, point_weight):
    seqs, bins, kernel_width = inputs.shape
    half_kernel_span = point_weight.shape[1]
    x = inputs.astype(jnp.float32)
    scale = lax.rsqrt(lax.optimization_barrier(jnp.mean(x * x, axis=-1, keepdims=True)) + 1e-06)
    normed = x * scale
    input_activations = gelu_value(normed).astype(jnp.bfloat16)
    flat_acts = input_activations.reshape(-1, kernel_width)
    hidden_state = jnp.dot(shifted_bin_rows(input_activations, DILATION_BINS).reshape(-1, kernel_width), dilated_kernel_weight[:, 0, :], preferred_element_type=jnp.float32)
    hidden_state = hidden_state + jnp.dot(flat_acts, dilated_kernel_weight[:, 1, :], preferred_element_type=jnp.float32)
    hidden_state = hidden_state + jnp.dot(shifted_bin_rows(input_activations, -DILATION_BINS).reshape(-1, kernel_width), dilated_kernel_weight[:, 2, :], preferred_element_type=jnp.float32)
    mid = gelu_value(hidden_state).astype(jnp.bfloat16)
    mixed = jnp.dot(mid, point_weight.T, preferred_element_type=jnp.float32)
    outputs = (x.reshape(-1, kernel_width) + mixed).astype(jnp.bfloat16).reshape(seqs, bins, kernel_width)
    flat_cot = cotangent.reshape(-1, kernel_width)
    back_mid = jnp.dot(flat_cot, point_weight, preferred_element_type=jnp.float32)
    hidden_state_gradient = (back_mid * gelu_slope(hidden_state)).astype(jnp.bfloat16).reshape(seqs, bins, half_kernel_span)
    stacked_tap_inputs = jnp.concatenate([shifted_bin_rows(hidden_state_gradient, -DILATION_BINS), hidden_state_gradient, shifted_bin_rows(hidden_state_gradient, DILATION_BINS)], axis=-1).reshape(-1, 3 * half_kernel_span)
    norm_factor = 1.0 / math.sqrt(seqs * bins)
    grad_point = jnp.dot(flat_cot.T, mid, preferred_element_type=jnp.float32) * norm_factor
    grad_conv = jnp.dot(flat_acts.T, stacked_tap_inputs, preferred_element_type=jnp.float32).reshape(kernel_width, 3, half_kernel_span) * norm_factor
    grad_acts = jnp.dot(stacked_tap_inputs, dilated_kernel_weight.reshape(kernel_width, 3 * half_kernel_span).T, preferred_element_type=jnp.float32)
    grad_normed = grad_acts.reshape(seqs, bins, kernel_width) * gelu_slope(normed)
    inner = lax.optimization_barrier(jnp.mean(grad_normed * x, axis=-1, keepdims=True))
    grad_inputs = cotangent.astype(jnp.float32) + scale * (grad_normed - x * scale * scale * inner)
    return (outputs, grad_inputs.astype(jnp.bfloat16), grad_conv, grad_point)
```

```python
import math

import jax
import jax.numpy as jnp
from jax import lax
from jax.sharding import PartitionSpec as P


def shifted(x, axis, by):
    peers = lax.axis_size(axis)
    pairs = [(i, i + by) for i in range(peers) if 0 <= i + by < peers]
    return lax.ppermute(x, axis, pairs)

AX = ("seq", "fsdp")
SIZES = {"y_lo": 2, "x": 4, "z": 8, "y_hi": 2, "core": 2}
GATHER_ORDER = ("y_hi", "core", "y_lo", "x", "z")


def coords_of(d):
    s, f = divmod(d, 4)
    return {"y_lo": s // 32, "x": (s // 8) % 4, "z": s % 8, "y_hi": f // 2, "core": f % 2}


def index_of(c):
    s = (c["y_lo"] * 4 + c["x"]) * 8 + c["z"]
    return s * 4 + c["y_hi"] * 2 + c["core"]


def ring_pairs(axis, step):
    pairs = []
    for d in range(64 * 4):
        c = dict(coords_of(d))
        c[axis] = (c[axis] + step) % SIZES[axis]
        pairs.append((d, index_of(c)))
    return pairs


def my_coord(axis):
    s = lax.axis_index("seq")
    f = lax.axis_index("fsdp")
    return {
        "y_lo": s // 32,
        "x": (s // 8) % 4,
        "z": s % 8,
        "y_hi": f // 2,
        "core": f % 2,
    }[axis]


def rs_stage(x, names, axis):
    n = SIZES[axis]
    i = my_coord(axis)
    dim = names.index(axis)

    def take(tgt):
        return lax.dynamic_index_in_dim(x, tgt, dim, keepdims=False)

    total = take(i)
    if n == 2:
        total = total + lax.ppermute(take(1 - i), AX, ring_pairs(axis, 1))
    else:
        h = n // 2
        g = n - 1 - h
        fwd = None
        for t in range(h):
            c = take((i + h - t + n) % n)
            fwd = lax.ppermute(c if fwd is None else c + fwd, AX, ring_pairs(axis, 1))
        bwd = None
        for t in range(g):
            c = take((i - g + t + n) % n)
            bwd = lax.ppermute(c if bwd is None else c + bwd, AX, ring_pairs(axis, -1))
        total = total + fwd
        if bwd is not None:
            total = total + bwd
    return total, [a for a in names if a != axis]


def ag_stage(x, names, axis):
    n = SIZES[axis]
    i = my_coord(axis)
    blocks = [(0, x)]
    if n == 2:
        blocks.append((1, lax.ppermute(x, AX, ring_pairs(axis, 1))))
    else:
        h = n // 2
        g = n - 1 - h
        cur = x
        for t in range(h):
            cur = lax.ppermute(cur, AX, ring_pairs(axis, 1))
            blocks.append((-(t + 1), cur))
        cur = x
        for t in range(g):
            cur = lax.ppermute(cur, AX, ring_pairs(axis, -1))
            blocks.append((t + 1, cur))
    new_names = [a for a in GATHER_ORDER if a in names or a == axis]
    pos = new_names.index(axis)
    shape = list(x.shape)
    shape.insert(pos, n)
    out = jnp.zeros(shape, x.dtype)
    for off, b in blocks:
        src = (i + off + n) % n
        out = lax.dynamic_update_slice_in_dim(out, jnp.expand_dims(b, pos), src, pos)
    return out, new_names


def gather_weights(block):
    names = []
    for axis in ("x", "y_hi", "z", "y_lo", "core"):
        block, names = ag_stage(block, names, axis)
    return block


def reduce_grads(part):
    names = list(GATHER_ORDER)
    for axis in ("core", "z", "x", "y_lo", "y_hi"):
        part, names = rs_stage(part, names, axis)
    return part


def gelu_value(v):
    return 0.5 * v * (1.0 + lax.erf(v * (1.0 / math.sqrt(2.0))))


def gelu_slope(v):
    return 0.5 * (1.0 + lax.erf(v * (1.0 / math.sqrt(2.0)))) + v * jnp.exp(-0.5 * v * v) * (
        1.0 / math.sqrt(2.0 * math.pi)
    )


def contract_rows(left, right):
    return lax.dot_general(
        left, right, (((0,), (0,)), ((), ())), preferred_element_type=jnp.float32
    )


def body(inputs, cotangent, dilated_kernel_weight, point_weight):
    seqs, bins, kernel_width = inputs.shape
    rows_all = seqs * bins * lax.axis_size("seq") * lax.axis_size("fsdp")
    norm_factor = 1.0 / math.sqrt(rows_all)
    rows, _, span = dilated_kernel_weight.shape
    block = jnp.concatenate([dilated_kernel_weight, point_weight[:, None, :]], axis=1)
    gathered = gather_weights(block.reshape(rows, 4 * span))
    fsdp_n = lax.axis_size("fsdp")
    full_w = (
        gathered.reshape(fsdp_n, kernel_width, 4, span)
        .transpose(1, 2, 0, 3)
        .reshape(kernel_width, 4, fsdp_n * span)
    )
    full_conv = full_w[:, 0:3, :]
    full_point = full_w[:, 3, :]
    half_kernel_span = full_point.shape[1]
    x = inputs.astype(jnp.float32)
    scale = lax.rsqrt(jnp.mean(x * x, axis=-1, keepdims=True) + 1e-06)
    normed = x * scale
    input_activations = gelu_value(normed).astype(jnp.bfloat16)
    flat_acts = input_activations.reshape(-1, kernel_width)
    acts_back = shifted(input_activations, ("seq", "fsdp"), 2)
    acts_ahead = shifted(input_activations, ("seq", "fsdp"), -2)
    hidden_state = jnp.dot(flat_acts, full_conv[:, 1, :], preferred_element_type=jnp.float32)
    hidden_state = hidden_state + jnp.dot(
        acts_back.reshape(-1, kernel_width), full_conv[:, 0, :], preferred_element_type=jnp.float32
    )
    hidden_state = hidden_state + jnp.dot(
        acts_ahead.reshape(-1, kernel_width), full_conv[:, 2, :], preferred_element_type=jnp.float32
    )
    mid = gelu_value(hidden_state).astype(jnp.bfloat16)
    mixed = lax.dot_general(
        mid, full_point, (((1,), (1,)), ((), ())), preferred_element_type=jnp.float32
    )
    outputs = (
        (x.reshape(-1, kernel_width) + mixed).astype(jnp.bfloat16).reshape(seqs, bins, kernel_width)
    )
    flat_cot = cotangent.reshape(-1, kernel_width)
    back_mid = jnp.dot(flat_cot, full_point, preferred_element_type=jnp.float32)
    hidden_state_gradient = (
        (back_mid * gelu_slope(hidden_state))
        .astype(jnp.bfloat16)
        .reshape(seqs, bins, half_kernel_span)
    )
    grad_later = shifted(hidden_state_gradient, ("seq", "fsdp"), -2)
    grad_earlier = shifted(hidden_state_gradient, ("seq", "fsdp"), 2)
    stacked_tap_inputs = jnp.concatenate(
        [grad_later, hidden_state_gradient, grad_earlier], axis=-1
    ).reshape(-1, 3 * half_kernel_span)
    grad_acts = lax.dot_general(
        stacked_tap_inputs,
        full_conv.reshape(kernel_width, 3 * half_kernel_span),
        (((1,), (1,)), ((), ())),
        preferred_element_type=jnp.float32,
    )
    grad_normed = grad_acts.reshape(seqs, bins, kernel_width) * gelu_slope(normed)
    inner = jnp.mean(grad_normed * x, axis=-1, keepdims=True)
    grad_inputs = (
        cotangent.astype(jnp.float32) + scale * (grad_normed - x * scale * scale * inner)
    ).astype(jnp.bfloat16)
    conv_part = contract_rows(flat_acts, stacked_tap_inputs)
    point_part = contract_rows(flat_cot, mid)
    whole = jnp.concatenate(
        [conv_part.reshape(kernel_width, 3, half_kernel_span), point_part[:, None, :]], axis=1
    )
    seq_n = lax.axis_size("seq")
    arranged = (
        whole.reshape(seq_n, rows, 4, fsdp_n, span)
        .transpose(3, 0, 1, 2, 4)
        .reshape(2, 2, 2, 4, 8, rows, 4 * span)
    )
    reduced = reduce_grads(arranged).reshape(rows, 4, span)
    grad_conv = reduced[:, 0:3, :] * norm_factor
    grad_point = reduced[:, 3, :] * norm_factor
    return (outputs, grad_inputs, grad_conv, grad_point)


def solution(mesh):
    return jax.shard_map(
        body,
        mesh=mesh,
        in_specs=(
            P(None, ("seq", "fsdp"), None),
            P(None, ("seq", "fsdp"), None),
            P("seq", None, "fsdp"),
            P("seq", "fsdp"),
        ),
        out_specs=(
            P(None, ("seq", "fsdp"), None),
            P(None, ("seq", "fsdp"), None),
            P("seq", None, "fsdp"),
            P("seq", "fsdp"),
        ),
        check_vma=False,
    )
```

```python
import math

import jax
import jax.numpy as jnp
from jax import lax
from jax.sharding import PartitionSpec as P


def shifted(x, axis, by):
    peers = lax.axis_size(axis)
    pairs = [(i, i + by) for i in range(peers) if 0 <= i + by < peers]
    return lax.ppermute(x, axis, pairs)

AX = ("seq", "fsdp")
SIZES = {"y_lo": 2, "x": 4, "z": 8, "y_hi": 2, "core": 2}
GATHER_ORDER = ("y_hi", "core", "y_lo", "x", "z")


def coords_of(d):
    s, f = divmod(d, 4)
    return {"y_lo": s // 32, "x": (s // 8) % 4, "z": s % 8, "y_hi": f // 2, "core": f % 2}


def index_of(c):
    s = (c["y_lo"] * 4 + c["x"]) * 8 + c["z"]
    return s * 4 + c["y_hi"] * 2 + c["core"]


def ring_pairs(axis, step):
    pairs = []
    for d in range(64 * 4):
        c = dict(coords_of(d))
        c[axis] = (c[axis] + step) % SIZES[axis]
        pairs.append((d, index_of(c)))
    return pairs


def my_coord(axis):
    s = lax.axis_index("seq")
    f = lax.axis_index("fsdp")
    return {
        "y_lo": s // 32,
        "x": (s // 8) % 4,
        "z": s % 8,
        "y_hi": f // 2,
        "core": f % 2,
    }[axis]


def rs_stage(x, axis, dim, blk):
    n = SIZES[axis]
    i = my_coord(axis)

    def take(tgt):
        return lax.dynamic_slice_in_dim(x, tgt * blk, blk, dim)

    total = take(i)
    if n == 2:
        total = total + lax.ppermute(take(1 - i), AX, ring_pairs(axis, 1))
    else:
        h = n // 2
        g = n - 1 - h
        fwd = None
        for t in range(h):
            c = take((i + h - t + n) % n)
            fwd = lax.ppermute(c if fwd is None else c + fwd, AX, ring_pairs(axis, 1))
        bwd = None
        for t in range(g):
            c = take((i - g + t + n) % n)
            bwd = lax.ppermute(c if bwd is None else c + bwd, AX, ring_pairs(axis, -1))
        total = total + fwd
        if bwd is not None:
            total = total + bwd
    return total


def ag_stage(x, axis, dim):
    n = SIZES[axis]
    i = my_coord(axis)
    blocks = [(0, x)]
    if n == 2:
        blocks.append((1, lax.ppermute(x, AX, ring_pairs(axis, 1))))
    else:
        h = n // 2
        g = n - 1 - h
        cur = x
        for t in range(h):
            cur = lax.ppermute(cur, AX, ring_pairs(axis, 1))
            blocks.append((-(t + 1), cur))
        cur = x
        for t in range(g):
            cur = lax.ppermute(cur, AX, ring_pairs(axis, -1))
            blocks.append((t + 1, cur))
    blk = x.shape[dim]
    shape = list(x.shape)
    shape[dim] = n * blk
    out = jnp.zeros(shape, x.dtype)
    for off, b in blocks:
        src = (i + off + n) % n
        out = lax.dynamic_update_slice_in_dim(out, b, src * blk, dim)
    return out


def gather_weights(block):
    for axis, dim in (("z", 1), ("x", 1), ("y_lo", 1), ("y_hi", 2), ("core", 2)):
        block = ag_stage(block, axis, dim)
    return block


def reduce_grads(part):
    taps, rows_all, cols_all = part.shape
    part = rs_stage(part, "core", 2, cols_all // 2)
    rows = rows_all // 64
    part = part.reshape(taps, 2, 4, 8, rows, cols_all // 2)
    for axis, dim in (("z", 3), ("x", 2), ("y_lo", 1)):
        part = rs_stage(part, axis, dim, 1)
    part = part.reshape(taps, rows, cols_all // 2)
    return rs_stage(part, "y_hi", 2, cols_all // 4)


def gelu_value(v):
    return 0.5 * v * (1.0 + lax.erf(v * (1.0 / math.sqrt(2.0))))


def gelu_slope(v):
    return 0.5 * (1.0 + lax.erf(v * (1.0 / math.sqrt(2.0)))) + v * jnp.exp(-0.5 * v * v) * (
        1.0 / math.sqrt(2.0 * math.pi)
    )


def contract_rows(left, right):
    return lax.dot_general(
        left, right, (((0,), (0,)), ((), ())), preferred_element_type=jnp.float32
    )


def body(inputs, cotangent, dilated_kernel_weight, point_weight):
    seqs, bins, kernel_width = inputs.shape
    rows_all = seqs * bins * lax.axis_size("seq") * lax.axis_size("fsdp")
    norm_factor = 1.0 / math.sqrt(rows_all)
    rows, taps, span = dilated_kernel_weight.shape
    block = jnp.concatenate([dilated_kernel_weight, point_weight[:, None, :]], axis=1)
    weights = gather_weights(block.transpose(1, 0, 2))
    half_kernel_span = weights.shape[2]
    x = inputs.astype(jnp.float32)
    scale = lax.rsqrt(jnp.mean(x * x, axis=-1, keepdims=True) + 1e-06)
    normed = x * scale
    input_activations = gelu_value(normed).astype(jnp.bfloat16)
    flat_acts = input_activations.reshape(-1, kernel_width)
    acts_back = shifted(input_activations, ("seq", "fsdp"), 2)
    acts_ahead = shifted(input_activations, ("seq", "fsdp"), -2)
    hidden_state = jnp.dot(flat_acts, weights[1], preferred_element_type=jnp.float32)
    hidden_state = hidden_state + jnp.dot(
        acts_back.reshape(-1, kernel_width), weights[0], preferred_element_type=jnp.float32
    )
    hidden_state = hidden_state + jnp.dot(
        acts_ahead.reshape(-1, kernel_width), weights[2], preferred_element_type=jnp.float32
    )
    mid = gelu_value(hidden_state).astype(jnp.bfloat16)
    mixed = lax.dot_general(
        mid, weights[3], (((1,), (1,)), ((), ())), preferred_element_type=jnp.float32
    )
    outputs = (
        (x.reshape(-1, kernel_width) + mixed).astype(jnp.bfloat16).reshape(seqs, bins, kernel_width)
    )
    flat_cot = cotangent.reshape(-1, kernel_width)
    back_mid = jnp.dot(flat_cot, weights[3], preferred_element_type=jnp.float32)
    hidden_state_gradient = (
        (back_mid * gelu_slope(hidden_state))
        .astype(jnp.bfloat16)
        .reshape(seqs, bins, half_kernel_span)
    )
    grad_later = shifted(hidden_state_gradient, ("seq", "fsdp"), -2)
    grad_earlier = shifted(hidden_state_gradient, ("seq", "fsdp"), 2)
    tap_inputs = [
        g.reshape(-1, half_kernel_span) for g in (grad_later, hidden_state_gradient, grad_earlier)
    ]
    grad_acts = None
    for k in range(taps):
        term = lax.dot_general(
            tap_inputs[k], weights[k], (((1,), (1,)), ((), ())), preferred_element_type=jnp.float32
        )
        grad_acts = term if grad_acts is None else grad_acts + term
    grad_normed = grad_acts.reshape(seqs, bins, kernel_width) * gelu_slope(normed)
    inner = jnp.mean(grad_normed * x, axis=-1, keepdims=True)
    grad_inputs = (
        cotangent.astype(jnp.float32) + scale * (grad_normed - x * scale * scale * inner)
    ).astype(jnp.bfloat16)
    parts = [contract_rows(flat_acts, t) for t in tap_inputs]
    parts.append(contract_rows(flat_cot, mid))
    reduced = reduce_grads(jnp.stack(parts, axis=0))
    grad_conv = reduced[0:taps].transpose(1, 0, 2) * norm_factor
    grad_point = reduced[taps] * norm_factor
    return (outputs, grad_inputs, grad_conv, grad_point)


def solution(mesh):
    return jax.shard_map(
        body,
        mesh=mesh,
        in_specs=(
            P(None, ("seq", "fsdp"), None),
            P(None, ("seq", "fsdp"), None),
            P("seq", None, "fsdp"),
            P("seq", "fsdp"),
        ),
        out_specs=(
            P(None, ("seq", "fsdp"), None),
            P(None, ("seq", "fsdp"), None),
            P("seq", None, "fsdp"),
            P("seq", "fsdp"),
        ),
        check_vma=False,
    )
```

```python
import math

import jax
import jax.numpy as jnp
from jax import lax
from jax.sharding import PartitionSpec as P


def shifted(x, axis, by):
    peers = lax.axis_size(axis)
    pairs = [(i, i + by) for i in range(peers) if 0 <= i + by < peers]
    return lax.ppermute(x, axis, pairs)

AX = ("seq", "fsdp")
SIZES = {"y_lo": 2, "x": 4, "z": 8, "y_hi": 2, "core": 2}
GATHER_ORDER = ("y_hi", "core", "y_lo", "x", "z")


def coords_of(d):
    s, f = divmod(d, 4)
    return {"y_lo": s // 32, "x": (s // 8) % 4, "z": s % 8, "y_hi": f // 2, "core": f % 2}


def index_of(c):
    s = (c["y_lo"] * 4 + c["x"]) * 8 + c["z"]
    return s * 4 + c["y_hi"] * 2 + c["core"]


def ring_pairs(axis, step):
    pairs = []
    for d in range(64 * 4):
        c = dict(coords_of(d))
        c[axis] = (c[axis] + step) % SIZES[axis]
        pairs.append((d, index_of(c)))
    return pairs


def my_coord(axis):
    s = lax.axis_index("seq")
    f = lax.axis_index("fsdp")
    return {
        "y_lo": s // 32,
        "x": (s // 8) % 4,
        "z": s % 8,
        "y_hi": f // 2,
        "core": f % 2,
    }[axis]


def rs_stage(x, axis, dim, blk):
    n = SIZES[axis]
    i = my_coord(axis)

    def take(tgt):
        return lax.dynamic_slice_in_dim(x, tgt * blk, blk, dim)

    total = take(i)
    if n == 2:
        total = total + lax.ppermute(take(1 - i), AX, ring_pairs(axis, 1))
    else:
        h = n // 2
        g = n - 1 - h
        fwd = None
        bwd = None
        for t in range(h):
            c = take((i + h - t + n) % n)
            fwd_send = c if fwd is None else c + fwd
            if t < g:
                c = take((i - g + t + n) % n)
                bwd_send = c if bwd is None else c + bwd
                fwd_send, bwd_send = lax.optimization_barrier((fwd_send, bwd_send))
                bwd = lax.ppermute(bwd_send, AX, ring_pairs(axis, -1))
            fwd = lax.ppermute(fwd_send, AX, ring_pairs(axis, 1))
        total = total + fwd
        if bwd is not None:
            total = total + bwd
    return total


def ag_stage(x, axis, dim):
    n = SIZES[axis]
    i = my_coord(axis)
    blocks = [(0, x)]
    if n == 2:
        blocks.append((1, lax.ppermute(x, AX, ring_pairs(axis, 1))))
    else:
        h = n // 2
        g = n - 1 - h
        cur = x
        for t in range(h):
            cur = lax.ppermute(cur, AX, ring_pairs(axis, 1))
            blocks.append((-(t + 1), cur))
        cur = x
        for t in range(g):
            cur = lax.ppermute(cur, AX, ring_pairs(axis, -1))
            blocks.append((t + 1, cur))
    blk = x.shape[dim]
    shape = list(x.shape)
    shape[dim] = n * blk
    out = jnp.zeros(shape, x.dtype)
    for off, b in blocks:
        src = (i + off + n) % n
        out = lax.dynamic_update_slice_in_dim(out, b, src * blk, dim)
    return out


def gather_weights(block):
    for axis, dim in (("z", 1), ("x", 1), ("y_lo", 1), ("y_hi", 2), ("core", 2)):
        block = ag_stage(block, axis, dim)
    return block


def reduce_grads(part):
    taps, rows_all, cols_all = part.shape
    part = rs_stage(part, "core", 2, cols_all // 2)
    rows = rows_all // 64
    part = part.reshape(taps, 2, 4, 8, rows, cols_all // 2)
    for axis, dim in (("z", 3), ("x", 2), ("y_lo", 1)):
        part = rs_stage(part, axis, dim, 1)
    part = part.reshape(taps, rows, cols_all // 2)
    return rs_stage(part, "y_hi", 2, cols_all // 4)


def gelu_value(v):
    return 0.5 * v * (1.0 + lax.erf(v * (1.0 / math.sqrt(2.0))))


def gelu_slope(v):
    return 0.5 * (1.0 + lax.erf(v * (1.0 / math.sqrt(2.0)))) + v * jnp.exp(-0.5 * v * v) * (
        1.0 / math.sqrt(2.0 * math.pi)
    )


def contract_rows(left, right):
    return lax.dot_general(
        left, right, (((0,), (0,)), ((), ())), preferred_element_type=jnp.float32
    )


def body(inputs, cotangent, dilated_kernel_weight, point_weight):
    seqs, bins, kernel_width = inputs.shape
    rows_all = seqs * bins * lax.axis_size("seq") * lax.axis_size("fsdp")
    norm_factor = 1.0 / math.sqrt(rows_all)
    rows, taps, span = dilated_kernel_weight.shape
    block = jnp.concatenate([dilated_kernel_weight, point_weight[:, None, :]], axis=1)
    weights = gather_weights(block.transpose(1, 0, 2))
    half_kernel_span = weights.shape[2]
    x = inputs.astype(jnp.float32)
    scale = lax.rsqrt(jnp.mean(x * x, axis=-1, keepdims=True) + 1e-06)
    normed = x * scale
    input_activations = gelu_value(normed).astype(jnp.bfloat16)
    flat_acts = input_activations.reshape(-1, kernel_width)
    acts_back = shifted(input_activations, ("seq", "fsdp"), 2)
    acts_ahead = shifted(input_activations, ("seq", "fsdp"), -2)
    hidden_state = jnp.dot(flat_acts, weights[1], preferred_element_type=jnp.float32)
    hidden_state = hidden_state + jnp.dot(
        acts_back.reshape(-1, kernel_width), weights[0], preferred_element_type=jnp.float32
    )
    hidden_state = hidden_state + jnp.dot(
        acts_ahead.reshape(-1, kernel_width), weights[2], preferred_element_type=jnp.float32
    )
    mid = gelu_value(hidden_state).astype(jnp.bfloat16)
    mixed = lax.dot_general(
        mid, weights[3], (((1,), (1,)), ((), ())), preferred_element_type=jnp.float32
    )
    outputs = (
        (x.reshape(-1, kernel_width) + mixed).astype(jnp.bfloat16).reshape(seqs, bins, kernel_width)
    )
    flat_cot = cotangent.reshape(-1, kernel_width)
    back_mid = jnp.dot(flat_cot, weights[3], preferred_element_type=jnp.float32)
    hidden_state_gradient = (
        (back_mid * gelu_slope(hidden_state))
        .astype(jnp.bfloat16)
        .reshape(seqs, bins, half_kernel_span)
    )
    grad_later = shifted(hidden_state_gradient, ("seq", "fsdp"), -2)
    grad_earlier = shifted(hidden_state_gradient, ("seq", "fsdp"), 2)
    tap_inputs = [
        g.reshape(-1, half_kernel_span) for g in (grad_later, hidden_state_gradient, grad_earlier)
    ]
    grad_acts = None
    for k in range(taps):
        term = lax.dot_general(
            tap_inputs[k], weights[k], (((1,), (1,)), ((), ())), preferred_element_type=jnp.float32
        )
        grad_acts = term if grad_acts is None else grad_acts + term
    grad_normed = grad_acts.reshape(seqs, bins, kernel_width) * gelu_slope(normed)
    inner = jnp.mean(grad_normed * x, axis=-1, keepdims=True)
    grad_inputs = (
        cotangent.astype(jnp.float32) + scale * (grad_normed - x * scale * scale * inner)
    ).astype(jnp.bfloat16)
    parts = [contract_rows(flat_acts, t) for t in tap_inputs]
    parts.append(contract_rows(flat_cot, mid))
    reduced = reduce_grads(jnp.stack(parts, axis=0))
    grad_conv = reduced[0:taps].transpose(1, 0, 2) * norm_factor
    grad_point = reduced[taps] * norm_factor
    return (outputs, grad_inputs, grad_conv, grad_point)


def solution(mesh):
    return jax.shard_map(
        body,
        mesh=mesh,
        in_specs=(
            P(None, ("seq", "fsdp"), None),
            P(None, ("seq", "fsdp"), None),
            P("seq", None, "fsdp"),
            P("seq", "fsdp"),
        ),
        out_specs=(
            P(None, ("seq", "fsdp"), None),
            P(None, ("seq", "fsdp"), None),
            P("seq", None, "fsdp"),
            P("seq", "fsdp"),
        ),
        check_vma=False,
    )
```

```python
import math

import jax
import jax.numpy as jnp
from jax import lax
from jax.sharding import PartitionSpec as P


def shifted(x, axis, by):
    peers = lax.axis_size(axis)
    pairs = [(i, i + by) for i in range(peers) if 0 <= i + by < peers]
    return lax.ppermute(x, axis, pairs)

AX = ("seq", "fsdp")
SIZES = {"y_lo": 2, "x": 4, "z": 8, "y_hi": 2, "core": 2}
GATHER_ORDER = ("y_hi", "core", "y_lo", "x", "z")


def coords_of(d):
    s, f = divmod(d, 4)
    return {"y_lo": s // 32, "x": (s // 8) % 4, "z": s % 8, "y_hi": f // 2, "core": f % 2}


def index_of(c):
    s = (c["y_lo"] * 4 + c["x"]) * 8 + c["z"]
    return s * 4 + c["y_hi"] * 2 + c["core"]


def ring_pairs(axis, step):
    pairs = []
    for d in range(64 * 4):
        c = dict(coords_of(d))
        c[axis] = (c[axis] + step) % SIZES[axis]
        pairs.append((d, index_of(c)))
    return pairs


def my_coord(axis):
    s = lax.axis_index("seq")
    f = lax.axis_index("fsdp")
    return {
        "y_lo": s // 32,
        "x": (s // 8) % 4,
        "z": s % 8,
        "y_hi": f // 2,
        "core": f % 2,
    }[axis]


def rs_stage(x, axis, dim, blk):
    n = SIZES[axis]
    i = my_coord(axis)

    def take(tgt):
        return lax.dynamic_slice_in_dim(x, tgt * blk, blk, dim)

    total = take(i)
    if n == 2:
        total = total + lax.ppermute(take(1 - i), AX, ring_pairs(axis, 1))
    else:
        h = n // 2
        g = n - 1 - h
        fwd = None
        bwd = None
        for t in range(h):
            c = take((i + h - t + n) % n)
            fwd_send = c if fwd is None else c + fwd
            if t < g:
                c = take((i - g + t + n) % n)
                bwd_send = c if bwd is None else c + bwd
                fwd_send, bwd_send = lax.optimization_barrier((fwd_send, bwd_send))
                bwd = lax.ppermute(bwd_send, AX, ring_pairs(axis, -1))
            fwd = lax.ppermute(fwd_send, AX, ring_pairs(axis, 1))
        total = total + fwd
        if bwd is not None:
            total = total + bwd
    return total


def ag_stage(x, axis, dim):
    n = SIZES[axis]
    i = my_coord(axis)
    blocks = [(0, x)]
    if n == 2:
        blocks.append((1, lax.ppermute(x, AX, ring_pairs(axis, 1))))
    else:
        h = n // 2
        g = n - 1 - h
        cur = x
        for t in range(h):
            cur = lax.ppermute(cur, AX, ring_pairs(axis, 1))
            blocks.append((-(t + 1), cur))
        cur = x
        for t in range(g):
            cur = lax.ppermute(cur, AX, ring_pairs(axis, -1))
            blocks.append((t + 1, cur))
    blk = x.shape[dim]
    shape = list(x.shape)
    shape[dim] = n * blk
    out = jnp.zeros(shape, x.dtype)
    for off, b in blocks:
        src = (i + off + n) % n
        out = lax.dynamic_update_slice_in_dim(out, b, src * blk, dim)
    return out


def y_pairs(step):
    pairs = []
    for d in range(64 * 4):
        c = dict(coords_of(d))
        y = (c["y_hi"] * 2 + c["y_lo"] + step) % 4
        c["y_hi"], c["y_lo"] = y // 2, y % 2
        pairs.append((d, index_of(c)))
    return pairs


def ag_y(b):
    y = my_coord("y_hi") * 2 + my_coord("y_lo")
    taps, r, c = b.shape
    half = r // 2
    from_prev = lax.ppermute(b, AX, y_pairs(1))
    from_next = lax.ppermute(b, AX, y_pairs(-1))
    send_f, send_b = lax.optimization_barrier((from_prev[:, :half], from_next[:, half:]))
    far_first = lax.ppermute(send_f, AX, y_pairs(1))
    far_second = lax.ppermute(send_b, AX, y_pairs(-1))
    out = jnp.zeros((taps, 2 * r, 2 * c), b.dtype)
    for blk, src, row in (
        (b, y, 0),
        (from_prev, (y + 3) % 4, 0),
        (from_next, (y + 1) % 4, 0),
        (far_first, (y + 2) % 4, 0),
        (far_second, (y + 2) % 4, half),
    ):
        out = lax.dynamic_update_slice(out, blk, (0, (src % 2) * r + row, (src // 2) * c))
    return out


def gather_weights(block):
    for axis, dim in (("z", 1), ("x", 1)):
        block = ag_stage(block, axis, dim)
    block = ag_y(block)
    return ag_stage(block, "core", 2)


def reduce_grads(part):
    taps, rows_all, cols_all = part.shape
    part = rs_stage(part, "core", 2, cols_all // 2)
    rows = rows_all // 64
    part = part.reshape(taps, 2, 4, 8, rows, cols_all // 2)
    for axis, dim in (("z", 3), ("x", 2), ("y_lo", 1)):
        part = rs_stage(part, axis, dim, 1)
    part = part.reshape(taps, rows, cols_all // 2)
    return rs_stage(part, "y_hi", 2, cols_all // 4)


def gelu_value(v):
    return 0.5 * v * (1.0 + lax.erf(v * (1.0 / math.sqrt(2.0))))


def gelu_slope(v):
    return 0.5 * (1.0 + lax.erf(v * (1.0 / math.sqrt(2.0)))) + v * jnp.exp(-0.5 * v * v) * (
        1.0 / math.sqrt(2.0 * math.pi)
    )


def contract_rows(left, right):
    return lax.dot_general(
        left, right, (((0,), (0,)), ((), ())), preferred_element_type=jnp.float32
    )


def body(inputs, cotangent, dilated_kernel_weight, point_weight):
    seqs, bins, kernel_width = inputs.shape
    rows_all = seqs * bins * lax.axis_size("seq") * lax.axis_size("fsdp")
    norm_factor = 1.0 / math.sqrt(rows_all)
    rows, taps, span = dilated_kernel_weight.shape
    block = jnp.concatenate([dilated_kernel_weight, point_weight[:, None, :]], axis=1)
    weights = gather_weights(block.transpose(1, 0, 2))
    half_kernel_span = weights.shape[2]
    x = inputs.astype(jnp.float32)
    scale = lax.rsqrt(jnp.mean(x * x, axis=-1, keepdims=True) + 1e-06)
    normed = x * scale
    input_activations = gelu_value(normed).astype(jnp.bfloat16)
    flat_acts = input_activations.reshape(-1, kernel_width)
    acts_back = shifted(input_activations, ("seq", "fsdp"), 2)
    acts_ahead = shifted(input_activations, ("seq", "fsdp"), -2)
    hidden_state = jnp.dot(flat_acts, weights[1], preferred_element_type=jnp.float32)
    hidden_state = hidden_state + jnp.dot(
        acts_back.reshape(-1, kernel_width), weights[0], preferred_element_type=jnp.float32
    )
    hidden_state = hidden_state + jnp.dot(
        acts_ahead.reshape(-1, kernel_width), weights[2], preferred_element_type=jnp.float32
    )
    mid = gelu_value(hidden_state).astype(jnp.bfloat16)
    mixed = lax.dot_general(
        mid, weights[3], (((1,), (1,)), ((), ())), preferred_element_type=jnp.float32
    )
    outputs = (
        (x.reshape(-1, kernel_width) + mixed).astype(jnp.bfloat16).reshape(seqs, bins, kernel_width)
    )
    flat_cot = cotangent.reshape(-1, kernel_width)
    back_mid = jnp.dot(flat_cot, weights[3], preferred_element_type=jnp.float32)
    hidden_state_gradient = (
        (back_mid * gelu_slope(hidden_state))
        .astype(jnp.bfloat16)
        .reshape(seqs, bins, half_kernel_span)
    )
    grad_later = shifted(hidden_state_gradient, ("seq", "fsdp"), -2)
    grad_earlier = shifted(hidden_state_gradient, ("seq", "fsdp"), 2)
    tap_inputs = [
        g.reshape(-1, half_kernel_span) for g in (grad_later, hidden_state_gradient, grad_earlier)
    ]
    grad_acts = None
    for k in range(taps):
        term = lax.dot_general(
            tap_inputs[k], weights[k], (((1,), (1,)), ((), ())), preferred_element_type=jnp.float32
        )
        grad_acts = term if grad_acts is None else grad_acts + term
    grad_normed = grad_acts.reshape(seqs, bins, kernel_width) * gelu_slope(normed)
    inner = jnp.mean(grad_normed * x, axis=-1, keepdims=True)
    grad_inputs = (
        cotangent.astype(jnp.float32) + scale * (grad_normed - x * scale * scale * inner)
    ).astype(jnp.bfloat16)
    parts = [contract_rows(flat_acts, t) for t in tap_inputs]
    parts.append(contract_rows(flat_cot, mid))
    reduced = reduce_grads(jnp.stack(parts, axis=0))
    grad_conv = reduced[0:taps].transpose(1, 0, 2) * norm_factor
    grad_point = reduced[taps] * norm_factor
    return (outputs, grad_inputs, grad_conv, grad_point)


def solution(mesh):
    return jax.shard_map(
        body,
        mesh=mesh,
        in_specs=(
            P(None, ("seq", "fsdp"), None),
            P(None, ("seq", "fsdp"), None),
            P("seq", None, "fsdp"),
            P("seq", "fsdp"),
        ),
        out_specs=(
            P(None, ("seq", "fsdp"), None),
            P(None, ("seq", "fsdp"), None),
            P("seq", None, "fsdp"),
            P("seq", "fsdp"),
        ),
        check_vma=False,
    )
```

```python
import math

import jax
import jax.numpy as jnp
from jax import lax
from jax.sharding import PartitionSpec as P


def shifted(x, axis, by):
    peers = lax.axis_size(axis)
    pairs = [(i, i + by) for i in range(peers) if 0 <= i + by < peers]
    return lax.ppermute(x, axis, pairs)

AX = ("seq", "fsdp")
SIZES = {"y_lo": 2, "x": 4, "z": 8, "y_hi": 2, "core": 2}
GATHER_ORDER = ("y_hi", "core", "y_lo", "x", "z")


def coords_of(d):
    s, f = divmod(d, 4)
    return {"y_lo": s // 32, "x": (s // 8) % 4, "z": s % 8, "y_hi": f // 2, "core": f % 2}


def index_of(c):
    s = (c["y_lo"] * 4 + c["x"]) * 8 + c["z"]
    return s * 4 + c["y_hi"] * 2 + c["core"]


def ring_pairs(axis, step):
    pairs = []
    for d in range(64 * 4):
        c = dict(coords_of(d))
        c[axis] = (c[axis] + step) % SIZES[axis]
        pairs.append((d, index_of(c)))
    return pairs


def my_coord(axis):
    s = lax.axis_index("seq")
    f = lax.axis_index("fsdp")
    return {
        "y_lo": s // 32,
        "x": (s // 8) % 4,
        "z": s % 8,
        "y_hi": f // 2,
        "core": f % 2,
    }[axis]


def rs_stage(x, axis, dim, blk):
    n = SIZES[axis]
    i = my_coord(axis)

    def take(tgt):
        return lax.dynamic_slice_in_dim(x, tgt * blk, blk, dim)

    total = take(i)
    if n == 2:
        total = total + lax.ppermute(take(1 - i), AX, ring_pairs(axis, 1))
    else:
        h = n // 2
        g = n - 1 - h
        fwd = None
        bwd = None
        for t in range(h):
            c = take((i + h - t + n) % n)
            fwd_send = c if fwd is None else c + fwd
            if t < g:
                c = take((i - g + t + n) % n)
                bwd_send = c if bwd is None else c + bwd
                fwd_send, bwd_send = lax.optimization_barrier((fwd_send, bwd_send))
                bwd = lax.ppermute(bwd_send, AX, ring_pairs(axis, -1))
            fwd = lax.ppermute(fwd_send, AX, ring_pairs(axis, 1))
        total = total + fwd
        if bwd is not None:
            total = total + bwd
    return total


def ag_stage(x, axis, dim, tied=None):
    n = SIZES[axis]
    i = my_coord(axis)
    blocks = [(0, x)]
    if n == 2:
        blocks.append((1, lax.ppermute(x, AX, ring_pairs(axis, 1))))
    else:
        h = n // 2
        g = n - 1 - h
        cur = x
        for t in range(h):
            cur = lax.ppermute(cur, AX, ring_pairs(axis, 1))
            if t == 0 and tied is not None:
                cur, tied = lax.optimization_barrier((cur, tied))
            blocks.append((-(t + 1), cur))
        cur = x
        for t in range(g):
            cur = lax.ppermute(cur, AX, ring_pairs(axis, -1))
            blocks.append((t + 1, cur))
    blk = x.shape[dim]
    shape = list(x.shape)
    shape[dim] = n * blk
    out = jnp.zeros(shape, x.dtype)
    for off, b in blocks:
        src = (i + off + n) % n
        out = lax.dynamic_update_slice_in_dim(out, b, src * blk, dim)
    if tied is not None:
        return out, tied
    return out


def y_pairs(step):
    pairs = []
    for d in range(64 * 4):
        c = dict(coords_of(d))
        y = (c["y_hi"] * 2 + c["y_lo"] + step) % 4
        c["y_hi"], c["y_lo"] = y // 2, y % 2
        pairs.append((d, index_of(c)))
    return pairs


def ag_y(b):
    y = my_coord("y_hi") * 2 + my_coord("y_lo")
    taps, r, c = b.shape
    half = r // 2
    from_prev = lax.ppermute(b, AX, y_pairs(1))
    from_next = lax.ppermute(b, AX, y_pairs(-1))
    send_f, send_b = lax.optimization_barrier((from_prev[:, :half], from_next[:, half:]))
    far_first = lax.ppermute(send_f, AX, y_pairs(1))
    far_second = lax.ppermute(send_b, AX, y_pairs(-1))
    out = jnp.zeros((taps, 2 * r, 2 * c), b.dtype)
    for blk, src, row in (
        (b, y, 0),
        (from_prev, (y + 3) % 4, 0),
        (from_next, (y + 1) % 4, 0),
        (far_first, (y + 2) % 4, 0),
        (far_second, (y + 2) % 4, half),
    ):
        out = lax.dynamic_update_slice(out, blk, (0, (src % 2) * r + row, (src // 2) * c))
    return out


def gather_weights(block, tied):
    block, tied = ag_stage(block, "z", 1, tied)
    block = ag_stage(block, "x", 1)
    block = ag_y(block)
    return ag_stage(block, "core", 2), tied


def reduce_grads(part):
    taps, rows_all, cols_all = part.shape
    part = rs_stage(part, "core", 2, cols_all // 2)
    rows = rows_all // 64
    part = part.reshape(taps, 2, 4, 8, rows, cols_all // 2)
    for axis, dim in (("z", 3), ("x", 2), ("y_lo", 1)):
        part = rs_stage(part, axis, dim, 1)
    part = part.reshape(taps, rows, cols_all // 2)
    return rs_stage(part, "y_hi", 2, cols_all // 4)


def gelu_value(v):
    return 0.5 * v * (1.0 + lax.erf(v * (1.0 / math.sqrt(2.0))))


def gelu_slope(v):
    return 0.5 * (1.0 + lax.erf(v * (1.0 / math.sqrt(2.0)))) + v * jnp.exp(-0.5 * v * v) * (
        1.0 / math.sqrt(2.0 * math.pi)
    )


def contract_rows(left, right):
    return lax.dot_general(
        left, right, (((0,), (0,)), ((), ())), preferred_element_type=jnp.float32
    )


def body(inputs, cotangent, dilated_kernel_weight, point_weight):
    seqs, bins, kernel_width = inputs.shape
    rows_all = seqs * bins * lax.axis_size("seq") * lax.axis_size("fsdp")
    norm_factor = 1.0 / math.sqrt(rows_all)
    rows, taps, span = dilated_kernel_weight.shape
    block = jnp.concatenate([dilated_kernel_weight, point_weight[:, None, :]], axis=1)
    x = inputs.astype(jnp.float32)
    scale = lax.rsqrt(jnp.mean(x * x, axis=-1, keepdims=True) + 1e-06)
    normed = x * scale
    input_activations = gelu_value(normed).astype(jnp.bfloat16)
    flat_acts = input_activations.reshape(-1, kernel_width)
    acts_back = shifted(input_activations, ("seq", "fsdp"), 2)
    acts_ahead = shifted(input_activations, ("seq", "fsdp"), -2)
    weights, (acts_back, acts_ahead) = gather_weights(
        block.transpose(1, 0, 2), (acts_back, acts_ahead)
    )
    half_kernel_span = weights.shape[2]
    hidden_state = jnp.dot(flat_acts, weights[1], preferred_element_type=jnp.float32)
    hidden_state = hidden_state + jnp.dot(
        acts_back.reshape(-1, kernel_width), weights[0], preferred_element_type=jnp.float32
    )
    hidden_state = hidden_state + jnp.dot(
        acts_ahead.reshape(-1, kernel_width), weights[2], preferred_element_type=jnp.float32
    )
    mid = gelu_value(hidden_state).astype(jnp.bfloat16)
    mixed = lax.dot_general(
        mid, weights[3], (((1,), (1,)), ((), ())), preferred_element_type=jnp.float32
    )
    outputs = (
        (x.reshape(-1, kernel_width) + mixed).astype(jnp.bfloat16).reshape(seqs, bins, kernel_width)
    )
    flat_cot = cotangent.reshape(-1, kernel_width)
    back_mid = jnp.dot(flat_cot, weights[3], preferred_element_type=jnp.float32)
    hidden_state_gradient = (
        (back_mid * gelu_slope(hidden_state))
        .astype(jnp.bfloat16)
        .reshape(seqs, bins, half_kernel_span)
    )
    grad_later = shifted(hidden_state_gradient, ("seq", "fsdp"), -2)
    grad_earlier = shifted(hidden_state_gradient, ("seq", "fsdp"), 2)
    tap_inputs = [
        g.reshape(-1, half_kernel_span) for g in (grad_later, hidden_state_gradient, grad_earlier)
    ]
    grad_acts = None
    for k in range(taps):
        term = lax.dot_general(
            tap_inputs[k], weights[k], (((1,), (1,)), ((), ())), preferred_element_type=jnp.float32
        )
        grad_acts = term if grad_acts is None else grad_acts + term
    grad_normed = grad_acts.reshape(seqs, bins, kernel_width) * gelu_slope(normed)
    inner = jnp.mean(grad_normed * x, axis=-1, keepdims=True)
    grad_inputs = (
        cotangent.astype(jnp.float32) + scale * (grad_normed - x * scale * scale * inner)
    ).astype(jnp.bfloat16)
    parts = [contract_rows(flat_acts, t) for t in tap_inputs]
    parts.append(contract_rows(flat_cot, mid))
    reduced = reduce_grads(jnp.stack(parts, axis=0))
    grad_conv = reduced[0:taps].transpose(1, 0, 2) * norm_factor
    grad_point = reduced[taps] * norm_factor
    return (outputs, grad_inputs, grad_conv, grad_point)


def solution(mesh):
    return jax.shard_map(
        body,
        mesh=mesh,
        in_specs=(
            P(None, ("seq", "fsdp"), None),
            P(None, ("seq", "fsdp"), None),
            P("seq", None, "fsdp"),
            P("seq", "fsdp"),
        ),
        out_specs=(
            P(None, ("seq", "fsdp"), None),
            P(None, ("seq", "fsdp"), None),
            P("seq", None, "fsdp"),
            P("seq", "fsdp"),
        ),
        check_vma=False,
    )
```

```python
import math

import jax
import jax.numpy as jnp
from jax import lax
from jax.sharding import PartitionSpec as P


def shifted(x, axis, by):
    peers = lax.axis_size(axis)
    pairs = [(i, i + by) for i in range(peers) if 0 <= i + by < peers]
    return lax.ppermute(x, axis, pairs)

AX = ("seq", "fsdp")
SIZES = {"y_lo": 2, "x": 4, "z": 8, "y_hi": 2, "core": 2}
GATHER_ORDER = ("y_hi", "core", "y_lo", "x", "z")


def coords_of(d):
    s, f = divmod(d, 4)
    return {"y_lo": s // 32, "x": (s // 8) % 4, "z": s % 8, "y_hi": f // 2, "core": f % 2}


def index_of(c):
    s = (c["y_lo"] * 4 + c["x"]) * 8 + c["z"]
    return s * 4 + c["y_hi"] * 2 + c["core"]


def ring_pairs(axis, step):
    pairs = []
    for d in range(64 * 4):
        c = dict(coords_of(d))
        c[axis] = (c[axis] + step) % SIZES[axis]
        pairs.append((d, index_of(c)))
    return pairs


def my_coord(axis):
    s = lax.axis_index("seq")
    f = lax.axis_index("fsdp")
    return {
        "y_lo": s // 32,
        "x": (s // 8) % 4,
        "z": s % 8,
        "y_hi": f // 2,
        "core": f % 2,
    }[axis]


def rs_stage(x, axis, dim, blk):
    n = SIZES[axis]
    i = my_coord(axis)

    def take(tgt):
        return lax.dynamic_slice_in_dim(x, tgt * blk, blk, dim)

    total = take(i)
    if n == 2:
        total = total + lax.ppermute(take(1 - i), AX, ring_pairs(axis, 1))
    else:
        h = n // 2
        g = n - 1 - h
        fwd = None
        bwd = None
        for t in range(h):
            c = take((i + h - t + n) % n)
            fwd_send = c if fwd is None else c + fwd
            if t < g:
                c = take((i - g + t + n) % n)
                bwd_send = c if bwd is None else c + bwd
                fwd_send, bwd_send = lax.optimization_barrier((fwd_send, bwd_send))
                bwd = lax.ppermute(bwd_send, AX, ring_pairs(axis, -1))
            fwd = lax.ppermute(fwd_send, AX, ring_pairs(axis, 1))
        total = total + fwd
        if bwd is not None:
            total = total + bwd
    return total


def ag_stage(x, axis, dim):
    n = SIZES[axis]
    i = my_coord(axis)
    blocks = [(0, x)]
    if n == 2:
        blocks.append((1, lax.ppermute(x, AX, ring_pairs(axis, 1))))
    else:
        h = n // 2
        g = n - 1 - h
        cur = x
        for t in range(h):
            cur = lax.ppermute(cur, AX, ring_pairs(axis, 1))
            blocks.append((-(t + 1), cur))
        cur = x
        for t in range(g):
            cur = lax.ppermute(cur, AX, ring_pairs(axis, -1))
            blocks.append((t + 1, cur))
    blk = x.shape[dim]
    shape = list(x.shape)
    shape[dim] = n * blk
    out = jnp.zeros(shape, x.dtype)
    for off, b in blocks:
        src = (i + off + n) % n
        out = lax.dynamic_update_slice_in_dim(out, b, src * blk, dim)
    return out


def y_pairs(step):
    pairs = []
    for d in range(64 * 4):
        c = dict(coords_of(d))
        y = (c["y_hi"] * 2 + c["y_lo"] + step) % 4
        c["y_hi"], c["y_lo"] = y // 2, y % 2
        pairs.append((d, index_of(c)))
    return pairs


def ag_y(b):
    y = my_coord("y_hi") * 2 + my_coord("y_lo")
    taps, r, c = b.shape
    half = r // 2
    from_prev = lax.ppermute(b, AX, y_pairs(1))
    from_next = lax.ppermute(b, AX, y_pairs(-1))
    send_f, send_b = lax.optimization_barrier((from_prev[:, :half], from_next[:, half:]))
    far_first = lax.ppermute(send_f, AX, y_pairs(1))
    far_second = lax.ppermute(send_b, AX, y_pairs(-1))
    out = jnp.zeros((taps, 2 * r, 2 * c), b.dtype)
    for blk, src, row in (
        (b, y, 0),
        (from_prev, (y + 3) % 4, 0),
        (from_next, (y + 1) % 4, 0),
        (far_first, (y + 2) % 4, 0),
        (far_second, (y + 2) % 4, half),
    ):
        out = lax.dynamic_update_slice(out, blk, (0, (src % 2) * r + row, (src // 2) * c))
    return out


def gather_weights(block):
    for axis, dim in (("z", 1), ("x", 1)):
        block = ag_stage(block, axis, dim)
    block = ag_y(block)
    return ag_stage(block, "core", 2)


def reduce_grads(part):
    taps, rows_all, cols_half = part.shape
    rows = rows_all // 64
    part = part.reshape(taps, 2, 4, 8, rows, cols_half)
    for axis, dim in (("z", 3), ("x", 2), ("y_lo", 1)):
        part = rs_stage(part, axis, dim, 1)
    part = part.reshape(taps, rows, cols_half)
    return rs_stage(part, "y_hi", 2, cols_half // 2)


def gelu_value(v):
    return 0.5 * v * (1.0 + lax.erf(v * (1.0 / math.sqrt(2.0))))


def gelu_slope(v):
    return 0.5 * (1.0 + lax.erf(v * (1.0 / math.sqrt(2.0)))) + v * jnp.exp(-0.5 * v * v) * (
        1.0 / math.sqrt(2.0 * math.pi)
    )


def contract_rows(left, right):
    return lax.dot_general(
        left, right, (((0,), (0,)), ((), ())), preferred_element_type=jnp.float32
    )


def body(inputs, cotangent, dilated_kernel_weight, point_weight):
    seqs, bins, kernel_width = inputs.shape
    rows_all = seqs * bins * lax.axis_size("seq") * lax.axis_size("fsdp")
    norm_factor = 1.0 / math.sqrt(rows_all)
    rows, taps, span = dilated_kernel_weight.shape
    block = jnp.concatenate([dilated_kernel_weight, point_weight[:, None, :]], axis=1)
    weights = gather_weights(block.transpose(1, 0, 2))
    half_kernel_span = weights.shape[2]
    x = inputs.astype(jnp.float32)
    scale = lax.rsqrt(jnp.mean(x * x, axis=-1, keepdims=True) + 1e-06)
    normed = x * scale
    input_activations = gelu_value(normed).astype(jnp.bfloat16)
    flat_acts = input_activations.reshape(-1, kernel_width)
    acts_back = shifted(input_activations, ("seq", "fsdp"), 2)
    acts_ahead = shifted(input_activations, ("seq", "fsdp"), -2)
    hidden_state = jnp.dot(flat_acts, weights[1], preferred_element_type=jnp.float32)
    hidden_state = hidden_state + jnp.dot(
        acts_back.reshape(-1, kernel_width), weights[0], preferred_element_type=jnp.float32
    )
    hidden_state = hidden_state + jnp.dot(
        acts_ahead.reshape(-1, kernel_width), weights[2], preferred_element_type=jnp.float32
    )
    mid = gelu_value(hidden_state).astype(jnp.bfloat16)
    mixed = lax.dot_general(
        mid, weights[3], (((1,), (1,)), ((), ())), preferred_element_type=jnp.float32
    )
    outputs = (
        (x.reshape(-1, kernel_width) + mixed).astype(jnp.bfloat16).reshape(seqs, bins, kernel_width)
    )
    flat_cot = cotangent.reshape(-1, kernel_width)
    back_mid = jnp.dot(flat_cot, weights[3], preferred_element_type=jnp.float32)
    hidden_state_gradient = (
        (back_mid * gelu_slope(hidden_state))
        .astype(jnp.bfloat16)
        .reshape(seqs, bins, half_kernel_span)
    )
    grad_later = shifted(hidden_state_gradient, ("seq", "fsdp"), -2)
    grad_earlier = shifted(hidden_state_gradient, ("seq", "fsdp"), 2)
    tap_inputs = [
        g.reshape(-1, half_kernel_span) for g in (grad_later, hidden_state_gradient, grad_earlier)
    ]
    grad_acts = None
    for k in range(taps):
        term = lax.dot_general(
            tap_inputs[k], weights[k], (((1,), (1,)), ((), ())), preferred_element_type=jnp.float32
        )
        grad_acts = term if grad_acts is None else grad_acts + term
    grad_normed = grad_acts.reshape(seqs, bins, kernel_width) * gelu_slope(normed)
    inner = jnp.mean(grad_normed * x, axis=-1, keepdims=True)
    grad_inputs = (
        cotangent.astype(jnp.float32) + scale * (grad_normed - x * scale * scale * inner)
    ).astype(jnp.bfloat16)
    core = my_coord("core")
    half = half_kernel_span // 2
    lefts = jnp.stack([flat_acts, flat_cot], axis=0)
    rights = jnp.stack(tap_inputs + [mid], axis=0)
    mine = lax.dynamic_slice_in_dim(rights, core * half, half, 2)
    theirs = lax.dynamic_slice_in_dim(rights, (1 - core) * half, half, 2)
    core_pairs = ring_pairs("core", 1)
    lefts_in = lax.ppermute(lefts, AX, core_pairs)
    rights_in = lax.ppermute(theirs, AX, core_pairs)
    lefts_all = jnp.concatenate([lefts, lefts_in], axis=1)
    rights_all = jnp.concatenate([mine, rights_in], axis=1)
    parts = [contract_rows(lefts_all[0], rights_all[k]) for k in range(taps)]
    parts.append(contract_rows(lefts_all[1], rights_all[taps]))
    reduced = reduce_grads(jnp.stack(parts, axis=0))
    grad_conv = reduced[0:taps].transpose(1, 0, 2) * norm_factor
    grad_point = reduced[taps] * norm_factor
    return (outputs, grad_inputs, grad_conv, grad_point)


def solution(mesh):
    return jax.shard_map(
        body,
        mesh=mesh,
        in_specs=(
            P(None, ("seq", "fsdp"), None),
            P(None, ("seq", "fsdp"), None),
            P("seq", None, "fsdp"),
            P("seq", "fsdp"),
        ),
        out_specs=(
            P(None, ("seq", "fsdp"), None),
            P(None, ("seq", "fsdp"), None),
            P("seq", None, "fsdp"),
            P("seq", "fsdp"),
        ),
        check_vma=False,
    )
```

```python
import math

import jax
import jax.numpy as jnp
from jax import lax
from jax.sharding import PartitionSpec as P


def shifted(x, axis, by):
    peers = lax.axis_size(axis)
    pairs = [(i, i + by) for i in range(peers) if 0 <= i + by < peers]
    return lax.ppermute(x, axis, pairs)

AX = ("seq", "fsdp")
SIZES = {"y_lo": 2, "x": 4, "z": 8, "y_hi": 2, "core": 2}
GATHER_ORDER = ("y_hi", "core", "y_lo", "x", "z")


def coords_of(d):
    s, f = divmod(d, 4)
    return {"y_lo": s // 32, "x": (s // 8) % 4, "z": s % 8, "y_hi": f // 2, "core": f % 2}


def index_of(c):
    s = (c["y_lo"] * 4 + c["x"]) * 8 + c["z"]
    return s * 4 + c["y_hi"] * 2 + c["core"]


def ring_pairs(axis, step):
    pairs = []
    for d in range(64 * 4):
        c = dict(coords_of(d))
        c[axis] = (c[axis] + step) % SIZES[axis]
        pairs.append((d, index_of(c)))
    return pairs


def my_coord(axis):
    s = lax.axis_index("seq")
    f = lax.axis_index("fsdp")
    return {
        "y_lo": s // 32,
        "x": (s // 8) % 4,
        "z": s % 8,
        "y_hi": f // 2,
        "core": f % 2,
    }[axis]


def rs_stage(x, axis, dim, blk):
    n = SIZES[axis]
    i = my_coord(axis)

    def take(tgt):
        return lax.dynamic_slice_in_dim(x, tgt * blk, blk, dim)

    total = take(i)
    if n == 2:
        total = total + lax.ppermute(take(1 - i), AX, ring_pairs(axis, 1))
    else:
        h = n // 2
        fwd = None
        bwd = None
        sh = None
        for t in range(h):
            cf = take((i + h - t + n) % n)
            cb = take((i - h + t + n) % n)
            if t == 0:
                sh = cf.shape[0] // 2
                fwd_send, bwd_send = cf[:sh], cb[sh:]
            elif t == 1:
                fwd_send = jnp.concatenate([cf[:sh] + fwd, cf[sh:]], axis=0)
                bwd_send = jnp.concatenate([cb[:sh], cb[sh:] + bwd], axis=0)
            else:
                fwd_send, bwd_send = cf + fwd, cb + bwd
            fwd_send, bwd_send = lax.optimization_barrier((fwd_send, bwd_send))
            fwd = lax.ppermute(fwd_send, AX, ring_pairs(axis, 1))
            bwd = lax.ppermute(bwd_send, AX, ring_pairs(axis, -1))
        total = total + fwd + bwd
    return total


def ag_stage(x, axis, dim):
    n = SIZES[axis]
    i = my_coord(axis)
    blocks = [(0, x)]
    if n == 2:
        blocks.append((1, lax.ppermute(x, AX, ring_pairs(axis, 1))))
    else:
        h = n // 2
        g = n - 1 - h
        cur = x
        for t in range(h):
            cur = lax.ppermute(cur, AX, ring_pairs(axis, 1))
            blocks.append((-(t + 1), cur))
        cur = x
        for t in range(g):
            cur = lax.ppermute(cur, AX, ring_pairs(axis, -1))
            blocks.append((t + 1, cur))
    blk = x.shape[dim]
    shape = list(x.shape)
    shape[dim] = n * blk
    out = jnp.zeros(shape, x.dtype)
    for off, b in blocks:
        src = (i + off + n) % n
        out = lax.dynamic_update_slice_in_dim(out, b, src * blk, dim)
    return out


def y_pairs(step):
    pairs = []
    for d in range(64 * 4):
        c = dict(coords_of(d))
        y = (c["y_hi"] * 2 + c["y_lo"] + step) % 4
        c["y_hi"], c["y_lo"] = y // 2, y % 2
        pairs.append((d, index_of(c)))
    return pairs


def ag_y(b):
    y = my_coord("y_hi") * 2 + my_coord("y_lo")
    taps, r, c = b.shape
    half = r // 2
    from_prev = lax.ppermute(b, AX, y_pairs(1))
    from_next = lax.ppermute(b, AX, y_pairs(-1))
    send_f, send_b = lax.optimization_barrier((from_prev[:, :half], from_next[:, half:]))
    far_first = lax.ppermute(send_f, AX, y_pairs(1))
    far_second = lax.ppermute(send_b, AX, y_pairs(-1))
    out = jnp.zeros((taps, 2 * r, 2 * c), b.dtype)
    for blk, src, row in (
        (b, y, 0),
        (from_prev, (y + 3) % 4, 0),
        (from_next, (y + 1) % 4, 0),
        (far_first, (y + 2) % 4, 0),
        (far_second, (y + 2) % 4, half),
    ):
        out = lax.dynamic_update_slice(out, blk, (0, (src % 2) * r + row, (src // 2) * c))
    return out


def gather_weights(block):
    for axis, dim in (("z", 1), ("x", 1)):
        block = ag_stage(block, axis, dim)
    block = ag_y(block)
    return ag_stage(block, "core", 2)


def reduce_grads(part):
    taps, rows_all, cols_half = part.shape
    rows = rows_all // 64
    part = part.reshape(taps, 2, 4, 8, rows, cols_half)
    for axis, dim in (("z", 3), ("x", 2), ("y_lo", 1)):
        part = rs_stage(part, axis, dim, 1)
    part = part.reshape(taps, rows, cols_half)
    return rs_stage(part, "y_hi", 2, cols_half // 2)


def gelu_value(v):
    return 0.5 * v * (1.0 + lax.erf(v * (1.0 / math.sqrt(2.0))))


def gelu_slope(v):
    return 0.5 * (1.0 + lax.erf(v * (1.0 / math.sqrt(2.0)))) + v * jnp.exp(-0.5 * v * v) * (
        1.0 / math.sqrt(2.0 * math.pi)
    )


def contract_rows(left, right):
    return lax.dot_general(
        left, right, (((0,), (0,)), ((), ())), preferred_element_type=jnp.float32
    )


def body(inputs, cotangent, dilated_kernel_weight, point_weight):
    seqs, bins, kernel_width = inputs.shape
    rows_all = seqs * bins * lax.axis_size("seq") * lax.axis_size("fsdp")
    norm_factor = 1.0 / math.sqrt(rows_all)
    rows, taps, span = dilated_kernel_weight.shape
    block = jnp.concatenate([dilated_kernel_weight, point_weight[:, None, :]], axis=1)
    weights = gather_weights(block.transpose(1, 0, 2))
    half_kernel_span = weights.shape[2]
    x = inputs.astype(jnp.float32)
    scale = lax.rsqrt(jnp.mean(x * x, axis=-1, keepdims=True) + 1e-06)
    normed = x * scale
    input_activations = gelu_value(normed).astype(jnp.bfloat16)
    flat_acts = input_activations.reshape(-1, kernel_width)
    acts_back = shifted(input_activations, ("seq", "fsdp"), 2)
    acts_ahead = shifted(input_activations, ("seq", "fsdp"), -2)
    hidden_state = jnp.dot(flat_acts, weights[1], preferred_element_type=jnp.float32)
    hidden_state = hidden_state + jnp.dot(
        acts_back.reshape(-1, kernel_width), weights[0], preferred_element_type=jnp.float32
    )
    hidden_state = hidden_state + jnp.dot(
        acts_ahead.reshape(-1, kernel_width), weights[2], preferred_element_type=jnp.float32
    )
    mid = gelu_value(hidden_state).astype(jnp.bfloat16)
    mixed = lax.dot_general(
        mid, weights[3], (((1,), (1,)), ((), ())), preferred_element_type=jnp.float32
    )
    outputs = (
        (x.reshape(-1, kernel_width) + mixed).astype(jnp.bfloat16).reshape(seqs, bins, kernel_width)
    )
    flat_cot = cotangent.reshape(-1, kernel_width)
    back_mid = jnp.dot(flat_cot, weights[3], preferred_element_type=jnp.float32)
    hidden_state_gradient = (
        (back_mid * gelu_slope(hidden_state))
        .astype(jnp.bfloat16)
        .reshape(seqs, bins, half_kernel_span)
    )
    grad_later = shifted(hidden_state_gradient, ("seq", "fsdp"), -2)
    grad_earlier = shifted(hidden_state_gradient, ("seq", "fsdp"), 2)
    tap_inputs = [
        g.reshape(-1, half_kernel_span) for g in (grad_later, hidden_state_gradient, grad_earlier)
    ]
    grad_acts = None
    for k in range(taps):
        term = lax.dot_general(
            tap_inputs[k], weights[k], (((1,), (1,)), ((), ())), preferred_element_type=jnp.float32
        )
        grad_acts = term if grad_acts is None else grad_acts + term
    grad_normed = grad_acts.reshape(seqs, bins, kernel_width) * gelu_slope(normed)
    inner = jnp.mean(grad_normed * x, axis=-1, keepdims=True)
    grad_inputs = (
        cotangent.astype(jnp.float32) + scale * (grad_normed - x * scale * scale * inner)
    ).astype(jnp.bfloat16)
    core = my_coord("core")
    half = half_kernel_span // 2
    lefts = jnp.stack([flat_acts, flat_cot], axis=0)
    rights = jnp.stack(tap_inputs + [mid], axis=0)
    mine = lax.dynamic_slice_in_dim(rights, core * half, half, 2)
    theirs = lax.dynamic_slice_in_dim(rights, (1 - core) * half, half, 2)
    core_pairs = ring_pairs("core", 1)
    lefts_in = lax.ppermute(lefts, AX, core_pairs)
    rights_in = lax.ppermute(theirs, AX, core_pairs)
    lefts_all = jnp.concatenate([lefts, lefts_in], axis=1)
    rights_all = jnp.concatenate([mine, rights_in], axis=1)
    parts = [contract_rows(lefts_all[0], rights_all[k]) for k in range(taps)]
    parts.append(contract_rows(lefts_all[1], rights_all[taps]))
    reduced = reduce_grads(jnp.stack(parts, axis=0))
    grad_conv = reduced[0:taps].transpose(1, 0, 2) * norm_factor
    grad_point = reduced[taps] * norm_factor
    return (outputs, grad_inputs, grad_conv, grad_point)


def solution(mesh):
    return jax.shard_map(
        body,
        mesh=mesh,
        in_specs=(
            P(None, ("seq", "fsdp"), None),
            P(None, ("seq", "fsdp"), None),
            P("seq", None, "fsdp"),
            P("seq", "fsdp"),
        ),
        out_specs=(
            P(None, ("seq", "fsdp"), None),
            P(None, ("seq", "fsdp"), None),
            P("seq", None, "fsdp"),
            P("seq", "fsdp"),
        ),
        check_vma=False,
    )
```

```python
import math

import jax
import jax.numpy as jnp
from jax import lax
from jax.sharding import PartitionSpec as P


def shifted(x, axis, by):
    peers = lax.axis_size(axis)
    pairs = [(i, i + by) for i in range(peers) if 0 <= i + by < peers]
    return lax.ppermute(x, axis, pairs)

AX = ("seq", "fsdp")
SIZES = {"y_lo": 2, "x": 4, "z": 8, "y_hi": 2, "core": 2}
GATHER_ORDER = ("y_hi", "core", "y_lo", "x", "z")


def coords_of(d):
    s, f = divmod(d, 4)
    return {"y_lo": s // 32, "x": (s // 8) % 4, "z": s % 8, "y_hi": f // 2, "core": f % 2}


def index_of(c):
    s = (c["y_lo"] * 4 + c["x"]) * 8 + c["z"]
    return s * 4 + c["y_hi"] * 2 + c["core"]


def ring_pairs(axis, step):
    pairs = []
    for d in range(64 * 4):
        c = dict(coords_of(d))
        c[axis] = (c[axis] + step) % SIZES[axis]
        pairs.append((d, index_of(c)))
    return pairs


def my_coord(axis):
    s = lax.axis_index("seq")
    f = lax.axis_index("fsdp")
    return {
        "y_lo": s // 32,
        "x": (s // 8) % 4,
        "z": s % 8,
        "y_hi": f // 2,
        "core": f % 2,
    }[axis]


def rs_stage(x, axis, dim, blk):
    n = SIZES[axis]
    i = my_coord(axis)

    def take(tgt):
        return lax.dynamic_slice_in_dim(x, tgt * blk, blk, dim)

    total = take(i)
    if n == 2:
        total = total + lax.ppermute(take(1 - i), AX, ring_pairs(axis, 1))
    else:
        h = n // 2
        fwd = None
        bwd = None
        sh = None
        for t in range(h):
            cf = take((i + h - t + n) % n)
            cb = take((i - h + t + n) % n)
            if t == 0:
                sh = cf.shape[0] // 2
                fwd_send, bwd_send = cf[:sh], cb[sh:]
            elif t == 1:
                fwd_send = jnp.concatenate([cf[:sh] + fwd, cf[sh:]], axis=0)
                bwd_send = jnp.concatenate([cb[:sh], cb[sh:] + bwd], axis=0)
            else:
                fwd_send, bwd_send = cf + fwd, cb + bwd
            fwd_send, bwd_send = lax.optimization_barrier((fwd_send, bwd_send))
            fwd = lax.ppermute(fwd_send, AX, ring_pairs(axis, 1))
            bwd = lax.ppermute(bwd_send, AX, ring_pairs(axis, -1))
        total = total + fwd + bwd
    return total


def ag_stage(x, axis, dim):
    n = SIZES[axis]
    i = my_coord(axis)
    blocks = [(0, x)]
    if n == 2:
        blocks.append((1, lax.ppermute(x, AX, ring_pairs(axis, 1))))
    else:
        h = n // 2
        g = n - 1 - h
        cur = x
        for t in range(h):
            cur = lax.ppermute(cur, AX, ring_pairs(axis, 1))
            blocks.append((-(t + 1), cur))
        cur = x
        for t in range(g):
            cur = lax.ppermute(cur, AX, ring_pairs(axis, -1))
            blocks.append((t + 1, cur))
    blk = x.shape[dim]
    shape = list(x.shape)
    shape[dim] = n * blk
    out = jnp.zeros(shape, x.dtype)
    for off, b in blocks:
        src = (i + off + n) % n
        out = lax.dynamic_update_slice_in_dim(out, b, src * blk, dim)
    return out


def y_pairs(step):
    pairs = []
    for d in range(64 * 4):
        c = dict(coords_of(d))
        y = (c["y_hi"] * 2 + c["y_lo"] + step) % 4
        c["y_hi"], c["y_lo"] = y // 2, y % 2
        pairs.append((d, index_of(c)))
    return pairs


def ag_y(b):
    y = my_coord("y_hi") * 2 + my_coord("y_lo")
    taps, r, c = b.shape
    half = r // 2
    from_prev = lax.ppermute(b, AX, y_pairs(1))
    from_next = lax.ppermute(b, AX, y_pairs(-1))
    send_f, send_b = lax.optimization_barrier((from_prev[:, :half], from_next[:, half:]))
    far_first = lax.ppermute(send_f, AX, y_pairs(1))
    far_second = lax.ppermute(send_b, AX, y_pairs(-1))
    out = jnp.zeros((taps, 2 * r, 2 * c), b.dtype)
    for blk, src, row in (
        (b, y, 0),
        (from_prev, (y + 3) % 4, 0),
        (from_next, (y + 1) % 4, 0),
        (far_first, (y + 2) % 4, 0),
        (far_second, (y + 2) % 4, half),
    ):
        out = lax.dynamic_update_slice(out, blk, (0, (src % 2) * r + row, (src // 2) * c))
    return out


def xor_pairs(axis, k):
    pairs = []
    for d in range(64 * 4):
        c = dict(coords_of(d))
        c[axis] = c[axis] ^ k
        pairs.append((d, index_of(c)))
    return pairs


def ag_doubling(x, axis, dim):
    n = SIZES[axis]
    i = my_coord(axis)
    k = 1
    while k < n:
        recv = lax.ppermute(x, AX, xor_pairs(axis, k))
        low = (i // k) % 2 == 0
        x = jnp.concatenate([jnp.where(low, x, recv), jnp.where(low, recv, x)], axis=dim)
        k *= 2
    return x


def gather_weights(block):
    for axis, dim in (("z", 1), ("x", 1)):
        block = ag_doubling(block, axis, dim)
    block = ag_y(block)
    return ag_stage(block, "core", 2)


def reduce_grads(part):
    taps, rows_all, cols_half = part.shape
    rows = rows_all // 64
    part = part.reshape(taps, 2, 4, 8, rows, cols_half)
    for axis, dim in (("z", 3), ("x", 2), ("y_lo", 1)):
        part = rs_stage(part, axis, dim, 1)
    part = part.reshape(taps, rows, cols_half)
    return rs_stage(part, "y_hi", 2, cols_half // 2)


def gelu_value(v):
    return 0.5 * v * (1.0 + lax.erf(v * (1.0 / math.sqrt(2.0))))


def gelu_slope(v):
    return 0.5 * (1.0 + lax.erf(v * (1.0 / math.sqrt(2.0)))) + v * jnp.exp(-0.5 * v * v) * (
        1.0 / math.sqrt(2.0 * math.pi)
    )


def contract_rows(left, right):
    return lax.dot_general(
        left, right, (((0,), (0,)), ((), ())), preferred_element_type=jnp.float32
    )


def body(inputs, cotangent, dilated_kernel_weight, point_weight):
    seqs, bins, kernel_width = inputs.shape
    rows_all = seqs * bins * lax.axis_size("seq") * lax.axis_size("fsdp")
    norm_factor = 1.0 / math.sqrt(rows_all)
    rows, taps, span = dilated_kernel_weight.shape
    block = jnp.concatenate([dilated_kernel_weight, point_weight[:, None, :]], axis=1)
    weights = gather_weights(block.transpose(1, 0, 2))
    half_kernel_span = weights.shape[2]
    x = inputs.astype(jnp.float32)
    scale = lax.rsqrt(jnp.mean(x * x, axis=-1, keepdims=True) + 1e-06)
    normed = x * scale
    input_activations = gelu_value(normed).astype(jnp.bfloat16)
    flat_acts = input_activations.reshape(-1, kernel_width)
    acts_back = shifted(input_activations, ("seq", "fsdp"), 2)
    acts_ahead = shifted(input_activations, ("seq", "fsdp"), -2)
    hidden_state = jnp.dot(flat_acts, weights[1], preferred_element_type=jnp.float32)
    hidden_state = hidden_state + jnp.dot(
        acts_back.reshape(-1, kernel_width), weights[0], preferred_element_type=jnp.float32
    )
    hidden_state = hidden_state + jnp.dot(
        acts_ahead.reshape(-1, kernel_width), weights[2], preferred_element_type=jnp.float32
    )
    mid = gelu_value(hidden_state).astype(jnp.bfloat16)
    mixed = lax.dot_general(
        mid, weights[3], (((1,), (1,)), ((), ())), preferred_element_type=jnp.float32
    )
    outputs = (
        (x.reshape(-1, kernel_width) + mixed).astype(jnp.bfloat16).reshape(seqs, bins, kernel_width)
    )
    flat_cot = cotangent.reshape(-1, kernel_width)
    back_mid = jnp.dot(flat_cot, weights[3], preferred_element_type=jnp.float32)
    hidden_state_gradient = (
        (back_mid * gelu_slope(hidden_state))
        .astype(jnp.bfloat16)
        .reshape(seqs, bins, half_kernel_span)
    )
    grad_later = shifted(hidden_state_gradient, ("seq", "fsdp"), -2)
    grad_earlier = shifted(hidden_state_gradient, ("seq", "fsdp"), 2)
    tap_inputs = [
        g.reshape(-1, half_kernel_span) for g in (grad_later, hidden_state_gradient, grad_earlier)
    ]
    grad_acts = None
    for k in range(taps):
        term = lax.dot_general(
            tap_inputs[k], weights[k], (((1,), (1,)), ((), ())), preferred_element_type=jnp.float32
        )
        grad_acts = term if grad_acts is None else grad_acts + term
    grad_normed = grad_acts.reshape(seqs, bins, kernel_width) * gelu_slope(normed)
    inner = jnp.mean(grad_normed * x, axis=-1, keepdims=True)
    grad_inputs = (
        cotangent.astype(jnp.float32) + scale * (grad_normed - x * scale * scale * inner)
    ).astype(jnp.bfloat16)
    core = my_coord("core")
    half = half_kernel_span // 2
    lefts = jnp.stack([flat_acts, flat_cot], axis=0)
    rights = jnp.stack(tap_inputs + [mid], axis=0)
    mine = lax.dynamic_slice_in_dim(rights, core * half, half, 2)
    theirs = lax.dynamic_slice_in_dim(rights, (1 - core) * half, half, 2)
    core_pairs = ring_pairs("core", 1)
    lefts_in = lax.ppermute(lefts, AX, core_pairs)
    rights_in = lax.ppermute(theirs, AX, core_pairs)
    lefts_all = jnp.concatenate([lefts, lefts_in], axis=1)
    rights_all = jnp.concatenate([mine, rights_in], axis=1)
    parts = [contract_rows(lefts_all[0], rights_all[k]) for k in range(taps)]
    parts.append(contract_rows(lefts_all[1], rights_all[taps]))
    reduced = reduce_grads(jnp.stack(parts, axis=0))
    grad_conv = reduced[0:taps].transpose(1, 0, 2) * norm_factor
    grad_point = reduced[taps] * norm_factor
    return (outputs, grad_inputs, grad_conv, grad_point)


def solution(mesh):
    return jax.shard_map(
        body,
        mesh=mesh,
        in_specs=(
            P(None, ("seq", "fsdp"), None),
            P(None, ("seq", "fsdp"), None),
            P("seq", None, "fsdp"),
            P("seq", "fsdp"),
        ),
        out_specs=(
            P(None, ("seq", "fsdp"), None),
            P(None, ("seq", "fsdp"), None),
            P("seq", None, "fsdp"),
            P("seq", "fsdp"),
        ),
        check_vma=False,
    )
```

```python
import math

import jax
import jax.numpy as jnp
from jax import lax
from jax.sharding import PartitionSpec as P


def shifted(x, axis, by):
    peers = lax.axis_size(axis)
    pairs = [(i, i + by) for i in range(peers) if 0 <= i + by < peers]
    return lax.ppermute(x, axis, pairs)

AX = ("seq", "fsdp")
SIZES = {"y_lo": 2, "x": 4, "z": 8, "y_hi": 2, "core": 2}
GATHER_ORDER = ("y_hi", "core", "y_lo", "x", "z")


def coords_of(d):
    s, f = divmod(d, 4)
    return {"y_lo": s // 32, "x": (s // 8) % 4, "z": s % 8, "y_hi": f // 2, "core": f % 2}


def index_of(c):
    s = (c["y_lo"] * 4 + c["x"]) * 8 + c["z"]
    return s * 4 + c["y_hi"] * 2 + c["core"]


def ring_pairs(axis, step):
    pairs = []
    for d in range(64 * 4):
        c = dict(coords_of(d))
        c[axis] = (c[axis] + step) % SIZES[axis]
        pairs.append((d, index_of(c)))
    return pairs


def my_coord(axis):
    s = lax.axis_index("seq")
    f = lax.axis_index("fsdp")
    return {
        "y_lo": s // 32,
        "x": (s // 8) % 4,
        "z": s % 8,
        "y_hi": f // 2,
        "core": f % 2,
    }[axis]


def rs_stage(x, axis, dim, blk):
    n = SIZES[axis]
    i = my_coord(axis)

    def take(tgt):
        return lax.dynamic_slice_in_dim(x, tgt * blk, blk, dim)

    total = take(i)
    if n == 2:
        total = total + lax.ppermute(take(1 - i), AX, ring_pairs(axis, 1))
    else:
        h = n // 2
        fwd = None
        bwd = None
        sh = None
        for t in range(h):
            cf = take((i + h - t + n) % n)
            cb = take((i - h + t + n) % n)
            if t == 0:
                sh = cf.shape[0] // 2
                fwd_send, bwd_send = cf[:sh], cb[sh:]
            elif t == 1:
                fwd_send = jnp.concatenate([cf[:sh] + fwd, cf[sh:]], axis=0)
                bwd_send = jnp.concatenate([cb[:sh], cb[sh:] + bwd], axis=0)
            else:
                fwd_send, bwd_send = cf + fwd, cb + bwd
            fwd_send, bwd_send = lax.optimization_barrier((fwd_send, bwd_send))
            fwd = lax.ppermute(fwd_send, AX, ring_pairs(axis, 1))
            bwd = lax.ppermute(bwd_send, AX, ring_pairs(axis, -1))
        total = total + fwd + bwd
    return total


def ag_stage(x, axis, dim):
    n = SIZES[axis]
    i = my_coord(axis)
    blocks = [(0, x)]
    if n == 2:
        blocks.append((1, lax.ppermute(x, AX, ring_pairs(axis, 1))))
    else:
        h = n // 2
        g = n - 1 - h
        cur = x
        for t in range(h):
            cur = lax.ppermute(cur, AX, ring_pairs(axis, 1))
            blocks.append((-(t + 1), cur))
        cur = x
        for t in range(g):
            cur = lax.ppermute(cur, AX, ring_pairs(axis, -1))
            blocks.append((t + 1, cur))
    blk = x.shape[dim]
    by_offset = dict(((off + n) % n, b) for off, b in blocks)
    ordered = [by_offset[o] for o in range(n)]
    doubled = jnp.concatenate(ordered + ordered, axis=dim)
    return lax.dynamic_slice_in_dim(doubled, (n - i) * blk, n * blk, dim)


def y_pairs(step):
    pairs = []
    for d in range(64 * 4):
        c = dict(coords_of(d))
        y = (c["y_hi"] * 2 + c["y_lo"] + step) % 4
        c["y_hi"], c["y_lo"] = y // 2, y % 2
        pairs.append((d, index_of(c)))
    return pairs


def ag_y(b):
    y = my_coord("y_hi") * 2 + my_coord("y_lo")
    taps, r, c = b.shape
    half = r // 2
    from_prev = lax.ppermute(b, AX, y_pairs(1))
    from_next = lax.ppermute(b, AX, y_pairs(-1))
    send_f, send_b = lax.optimization_barrier((from_prev[:, :half], from_next[:, half:]))
    far_first = lax.ppermute(send_f, AX, y_pairs(1))
    far_second = lax.ppermute(send_b, AX, y_pairs(-1))
    out = jnp.zeros((taps, 2 * r, 2 * c), b.dtype)
    for blk, src, row in (
        (b, y, 0),
        (from_prev, (y + 3) % 4, 0),
        (from_next, (y + 1) % 4, 0),
        (far_first, (y + 2) % 4, 0),
        (far_second, (y + 2) % 4, half),
    ):
        out = lax.dynamic_update_slice(out, blk, (0, (src % 2) * r + row, (src // 2) * c))
    return out


def gather_weights(block):
    for axis, dim in (("z", 1), ("x", 1)):
        block = ag_stage(block, axis, dim)
    block = ag_y(block)
    return ag_stage(block, "core", 2)


def reduce_grads(part):
    taps, rows_all, cols_half = part.shape
    rows = rows_all // 64
    part = part.reshape(taps, 2, 4, 8, rows, cols_half)
    for axis, dim in (("z", 3), ("x", 2), ("y_lo", 1)):
        part = rs_stage(part, axis, dim, 1)
    part = part.reshape(taps, rows, cols_half)
    return rs_stage(part, "y_hi", 2, cols_half // 2)


def gelu_value(v):
    return 0.5 * v * (1.0 + lax.erf(v * (1.0 / math.sqrt(2.0))))


def gelu_slope(v):
    return 0.5 * (1.0 + lax.erf(v * (1.0 / math.sqrt(2.0)))) + v * jnp.exp(-0.5 * v * v) * (
        1.0 / math.sqrt(2.0 * math.pi)
    )


def contract_rows(left, right):
    return lax.dot_general(
        left, right, (((0,), (0,)), ((), ())), preferred_element_type=jnp.float32
    )


def body(inputs, cotangent, dilated_kernel_weight, point_weight):
    seqs, bins, kernel_width = inputs.shape
    rows_all = seqs * bins * lax.axis_size("seq") * lax.axis_size("fsdp")
    norm_factor = 1.0 / math.sqrt(rows_all)
    rows, taps, span = dilated_kernel_weight.shape
    block = jnp.concatenate([dilated_kernel_weight, point_weight[:, None, :]], axis=1)
    weights = gather_weights(block.transpose(1, 0, 2))
    half_kernel_span = weights.shape[2]
    x = inputs.astype(jnp.float32)
    scale = lax.rsqrt(jnp.mean(x * x, axis=-1, keepdims=True) + 1e-06)
    normed = x * scale
    input_activations = gelu_value(normed).astype(jnp.bfloat16)
    flat_acts = input_activations.reshape(-1, kernel_width)
    acts_back = shifted(input_activations, ("seq", "fsdp"), 2)
    acts_ahead = shifted(input_activations, ("seq", "fsdp"), -2)
    hidden_state = jnp.dot(flat_acts, weights[1], preferred_element_type=jnp.float32)
    hidden_state = hidden_state + jnp.dot(
        acts_back.reshape(-1, kernel_width), weights[0], preferred_element_type=jnp.float32
    )
    hidden_state = hidden_state + jnp.dot(
        acts_ahead.reshape(-1, kernel_width), weights[2], preferred_element_type=jnp.float32
    )
    mid = gelu_value(hidden_state).astype(jnp.bfloat16)
    mixed = lax.dot_general(
        mid, weights[3], (((1,), (1,)), ((), ())), preferred_element_type=jnp.float32
    )
    outputs = (
        (x.reshape(-1, kernel_width) + mixed).astype(jnp.bfloat16).reshape(seqs, bins, kernel_width)
    )
    flat_cot = cotangent.reshape(-1, kernel_width)
    back_mid = jnp.dot(flat_cot, weights[3], preferred_element_type=jnp.float32)
    hidden_state_gradient = (
        (back_mid * gelu_slope(hidden_state))
        .astype(jnp.bfloat16)
        .reshape(seqs, bins, half_kernel_span)
    )
    grad_later = shifted(hidden_state_gradient, ("seq", "fsdp"), -2)
    grad_earlier = shifted(hidden_state_gradient, ("seq", "fsdp"), 2)
    tap_inputs = [
        g.reshape(-1, half_kernel_span) for g in (grad_later, hidden_state_gradient, grad_earlier)
    ]
    grad_acts = None
    for k in range(taps):
        term = lax.dot_general(
            tap_inputs[k], weights[k], (((1,), (1,)), ((), ())), preferred_element_type=jnp.float32
        )
        grad_acts = term if grad_acts is None else grad_acts + term
    grad_normed = grad_acts.reshape(seqs, bins, kernel_width) * gelu_slope(normed)
    inner = jnp.mean(grad_normed * x, axis=-1, keepdims=True)
    grad_inputs = (
        cotangent.astype(jnp.float32) + scale * (grad_normed - x * scale * scale * inner)
    ).astype(jnp.bfloat16)
    core = my_coord("core")
    half = half_kernel_span // 2
    lefts = jnp.stack([flat_acts, flat_cot], axis=0)
    rights = jnp.stack(tap_inputs + [mid], axis=0)
    mine = lax.dynamic_slice_in_dim(rights, core * half, half, 2)
    theirs = lax.dynamic_slice_in_dim(rights, (1 - core) * half, half, 2)
    core_pairs = ring_pairs("core", 1)
    lefts_in = lax.ppermute(lefts, AX, core_pairs)
    rights_in = lax.ppermute(theirs, AX, core_pairs)
    lefts_all = jnp.concatenate([lefts, lefts_in], axis=1)
    rights_all = jnp.concatenate([mine, rights_in], axis=1)
    parts = [contract_rows(lefts_all[0], rights_all[k]) for k in range(taps)]
    parts.append(contract_rows(lefts_all[1], rights_all[taps]))
    reduced = reduce_grads(jnp.stack(parts, axis=0))
    grad_conv = reduced[0:taps].transpose(1, 0, 2) * norm_factor
    grad_point = reduced[taps] * norm_factor
    return (outputs, grad_inputs, grad_conv, grad_point)


def solution(mesh):
    return jax.shard_map(
        body,
        mesh=mesh,
        in_specs=(
            P(None, ("seq", "fsdp"), None),
            P(None, ("seq", "fsdp"), None),
            P("seq", None, "fsdp"),
            P("seq", "fsdp"),
        ),
        out_specs=(
            P(None, ("seq", "fsdp"), None),
            P(None, ("seq", "fsdp"), None),
            P("seq", None, "fsdp"),
            P("seq", "fsdp"),
        ),
        check_vma=False,
    )
```

```python
import math

import jax
import jax.numpy as jnp
from jax import lax
from jax.sharding import PartitionSpec as P


def shifted(x, axis, by):
    peers = lax.axis_size(axis)
    pairs = [(i, i + by) for i in range(peers) if 0 <= i + by < peers]
    return lax.ppermute(x, axis, pairs)

AX = ("seq", "fsdp")
SIZES = {"y_lo": 2, "x": 4, "z": 8, "y_hi": 2, "core": 2}
GATHER_ORDER = ("y_hi", "core", "y_lo", "x", "z")


def coords_of(d):
    s, f = divmod(d, 4)
    return {"y_lo": s // 32, "x": (s // 8) % 4, "z": s % 8, "y_hi": f // 2, "core": f % 2}


def index_of(c):
    s = (c["y_lo"] * 4 + c["x"]) * 8 + c["z"]
    return s * 4 + c["y_hi"] * 2 + c["core"]


def ring_pairs(axis, step):
    pairs = []
    for d in range(64 * 4):
        c = dict(coords_of(d))
        c[axis] = (c[axis] + step) % SIZES[axis]
        pairs.append((d, index_of(c)))
    return pairs


def my_coord(axis):
    s = lax.axis_index("seq")
    f = lax.axis_index("fsdp")
    return {
        "y_lo": s // 32,
        "x": (s // 8) % 4,
        "z": s % 8,
        "y_hi": f // 2,
        "core": f % 2,
    }[axis]


def rs_stage(x, axis, dim, blk):
    n = SIZES[axis]
    i = my_coord(axis)

    def take(tgt):
        return lax.dynamic_slice_in_dim(x, tgt * blk, blk, dim)

    total = take(i)
    if n == 2:
        total = total + lax.ppermute(take(1 - i), AX, ring_pairs(axis, 1))
    else:
        h = n // 2
        fwd = None
        bwd = None
        sh = None
        for t in range(h):
            cf = take((i + h - t + n) % n)
            cb = take((i - h + t + n) % n)
            if t == 0:
                sh = cf.shape[0] // 2
                fwd_send, bwd_send = cf[:sh], cb[sh:]
            elif t == 1:
                fwd_send = jnp.concatenate([cf[:sh] + fwd, cf[sh:]], axis=0)
                bwd_send = jnp.concatenate([cb[:sh], cb[sh:] + bwd], axis=0)
            else:
                fwd_send, bwd_send = cf + fwd, cb + bwd
            fwd_send, bwd_send = lax.optimization_barrier((fwd_send, bwd_send))
            fwd = lax.ppermute(fwd_send, AX, ring_pairs(axis, 1))
            bwd = lax.ppermute(bwd_send, AX, ring_pairs(axis, -1))
        total = total + fwd + bwd
    return total


def ag_stage(x, axis, dim):
    n = SIZES[axis]
    i = my_coord(axis)
    blocks = [(0, x)]
    if n == 2:
        blocks.append((1, lax.ppermute(x, AX, ring_pairs(axis, 1))))
    else:
        h = n // 2
        g = n - 1 - h
        cur = x
        for t in range(h):
            cur = lax.ppermute(cur, AX, ring_pairs(axis, 1))
            blocks.append((-(t + 1), cur))
        cur = x
        for t in range(g):
            cur = lax.ppermute(cur, AX, ring_pairs(axis, -1))
            blocks.append((t + 1, cur))
    blk = x.shape[dim]
    by_offset = dict(((off + n) % n, b) for off, b in blocks)
    ordered = [by_offset[o] for o in range(n)]
    doubled = jnp.concatenate(ordered + ordered, axis=dim)
    return lax.dynamic_slice_in_dim(doubled, (n - i) * blk, n * blk, dim)


def y_pairs(step):
    pairs = []
    for d in range(64 * 4):
        c = dict(coords_of(d))
        y = (c["y_hi"] * 2 + c["y_lo"] + step) % 4
        c["y_hi"], c["y_lo"] = y // 2, y % 2
        pairs.append((d, index_of(c)))
    return pairs


def ag_y(b):
    y = my_coord("y_hi") * 2 + my_coord("y_lo")
    taps, r, c = b.shape
    half = r // 2
    from_prev = lax.ppermute(b, AX, y_pairs(1))
    from_next = lax.ppermute(b, AX, y_pairs(-1))
    send_f, send_b = lax.optimization_barrier((from_prev[:, :half], from_next[:, half:]))
    far_first = lax.ppermute(send_f, AX, y_pairs(1))
    far_second = lax.ppermute(send_b, AX, y_pairs(-1))
    far = jnp.concatenate([far_first, far_second], axis=1)
    by_offset = jnp.stack([b, from_next, far, from_prev], axis=0)
    by_source = lax.dynamic_slice_in_dim(
        jnp.concatenate([by_offset, by_offset], axis=0), 4 - y, 4, 0
    )
    return jnp.concatenate(
        [
            jnp.concatenate([by_source[0], by_source[1]], axis=1),
            jnp.concatenate([by_source[2], by_source[3]], axis=1),
        ],
        axis=2,
    )


def gather_weights(block):
    for axis, dim in (("z", 1), ("x", 1)):
        block = ag_stage(block, axis, dim)
    block = ag_y(block)
    return ag_stage(block, "core", 2)


def reduce_grads(part):
    taps, rows_all, cols_half = part.shape
    rows = rows_all // 64
    part = part.reshape(taps, 2, 4, 8, rows, cols_half)
    for axis, dim in (("z", 3), ("x", 2), ("y_lo", 1)):
        part = rs_stage(part, axis, dim, 1)
    part = part.reshape(taps, rows, cols_half)
    return rs_stage(part, "y_hi", 2, cols_half // 2)


def gelu_value(v):
    return 0.5 * v * (1.0 + lax.erf(v * (1.0 / math.sqrt(2.0))))


def gelu_slope(v):
    return 0.5 * (1.0 + lax.erf(v * (1.0 / math.sqrt(2.0)))) + v * jnp.exp(-0.5 * v * v) * (
        1.0 / math.sqrt(2.0 * math.pi)
    )


def contract_rows(left, right):
    return lax.dot_general(
        left, right, (((0,), (0,)), ((), ())), preferred_element_type=jnp.float32
    )


def body(inputs, cotangent, dilated_kernel_weight, point_weight):
    seqs, bins, kernel_width = inputs.shape
    rows_all = seqs * bins * lax.axis_size("seq") * lax.axis_size("fsdp")
    norm_factor = 1.0 / math.sqrt(rows_all)
    rows, taps, span = dilated_kernel_weight.shape
    block = jnp.concatenate([dilated_kernel_weight, point_weight[:, None, :]], axis=1)
    weights = gather_weights(block.transpose(1, 0, 2))
    half_kernel_span = weights.shape[2]
    x = inputs.astype(jnp.float32)
    scale = lax.rsqrt(jnp.mean(x * x, axis=-1, keepdims=True) + 1e-06)
    normed = x * scale
    input_activations = gelu_value(normed).astype(jnp.bfloat16)
    flat_acts = input_activations.reshape(-1, kernel_width)
    acts_back = shifted(input_activations, ("seq", "fsdp"), 2)
    acts_ahead = shifted(input_activations, ("seq", "fsdp"), -2)
    hidden_state = jnp.dot(flat_acts, weights[1], preferred_element_type=jnp.float32)
    hidden_state = hidden_state + jnp.dot(
        acts_back.reshape(-1, kernel_width), weights[0], preferred_element_type=jnp.float32
    )
    hidden_state = hidden_state + jnp.dot(
        acts_ahead.reshape(-1, kernel_width), weights[2], preferred_element_type=jnp.float32
    )
    mid = gelu_value(hidden_state).astype(jnp.bfloat16)
    mixed = lax.dot_general(
        mid, weights[3], (((1,), (1,)), ((), ())), preferred_element_type=jnp.float32
    )
    outputs = (
        (x.reshape(-1, kernel_width) + mixed).astype(jnp.bfloat16).reshape(seqs, bins, kernel_width)
    )
    flat_cot = cotangent.reshape(-1, kernel_width)
    back_mid = jnp.dot(flat_cot, weights[3], preferred_element_type=jnp.float32)
    hidden_state_gradient = (
        (back_mid * gelu_slope(hidden_state))
        .astype(jnp.bfloat16)
        .reshape(seqs, bins, half_kernel_span)
    )
    grad_later = shifted(hidden_state_gradient, ("seq", "fsdp"), -2)
    grad_earlier = shifted(hidden_state_gradient, ("seq", "fsdp"), 2)
    tap_inputs = [
        g.reshape(-1, half_kernel_span) for g in (grad_later, hidden_state_gradient, grad_earlier)
    ]
    grad_acts = None
    for k in range(taps):
        term = lax.dot_general(
            tap_inputs[k], weights[k], (((1,), (1,)), ((), ())), preferred_element_type=jnp.float32
        )
        grad_acts = term if grad_acts is None else grad_acts + term
    grad_normed = grad_acts.reshape(seqs, bins, kernel_width) * gelu_slope(normed)
    inner = jnp.mean(grad_normed * x, axis=-1, keepdims=True)
    grad_inputs = (
        cotangent.astype(jnp.float32) + scale * (grad_normed - x * scale * scale * inner)
    ).astype(jnp.bfloat16)
    core = my_coord("core")
    half = half_kernel_span // 2
    lefts = jnp.stack([flat_acts, flat_cot], axis=0)
    rights = jnp.stack(tap_inputs + [mid], axis=0)
    mine = lax.dynamic_slice_in_dim(rights, core * half, half, 2)
    theirs = lax.dynamic_slice_in_dim(rights, (1 - core) * half, half, 2)
    core_pairs = ring_pairs("core", 1)
    lefts_in = lax.ppermute(lefts, AX, core_pairs)
    rights_in = lax.ppermute(theirs, AX, core_pairs)
    lefts_all = jnp.concatenate([lefts, lefts_in], axis=1)
    rights_all = jnp.concatenate([mine, rights_in], axis=1)
    parts = [contract_rows(lefts_all[0], rights_all[k]) for k in range(taps)]
    parts.append(contract_rows(lefts_all[1], rights_all[taps]))
    reduced = reduce_grads(jnp.stack(parts, axis=0))
    grad_conv = reduced[0:taps].transpose(1, 0, 2) * norm_factor
    grad_point = reduced[taps] * norm_factor
    return (outputs, grad_inputs, grad_conv, grad_point)


def solution(mesh):
    return jax.shard_map(
        body,
        mesh=mesh,
        in_specs=(
            P(None, ("seq", "fsdp"), None),
            P(None, ("seq", "fsdp"), None),
            P("seq", None, "fsdp"),
            P("seq", "fsdp"),
        ),
        out_specs=(
            P(None, ("seq", "fsdp"), None),
            P(None, ("seq", "fsdp"), None),
            P("seq", None, "fsdp"),
            P("seq", "fsdp"),
        ),
        check_vma=False,
    )
```
